1024 devices in a mesh: grid: 256 (over y, x, z_hi, core), mode: 4 (over z_lo).
Axes of the slice: x: 4, y: 8, z: 16 (z_hi: 4, z_lo: 4; z = z_hi * 4 + z_lo), core: 2. Of those that a mesh axis runs over, the one named last changes fastest.
Arguments:
- modes: bfloat16 [16, 3, 512, 32, 128], P('mode', None, 'grid'), may hold values from -0.29882812 to 0.29882812
- eigenvalues: float32 [16], P('mode'), may hold values from 2 to 50
- density: float32 [512, 32, 128], P('grid'), may hold values from 0.1 to 1
Outputs:
- gradient: float32 [512, 32, 128], P('grid')
The draws below stay inside these ranges and needn't reach their ends.
All inputs are finite; a program needn't handle non-finite values.
Results may differ from the reference program's by a relative error of at most 0.006.
Values may be sent and summed in bfloat16 or wider, within the bound.
No kernel may reach another device: no remote copies, remote signals or barrier semaphores. Data moves between devices by JAX's collectives and lax.ppermute only.
A program may use at most 32 MiB of HBM per device.

```python
import math
import jax
import jax.numpy as jnp
import numpy as np
from jax import lax

EX = 128
EY = 32
MODES = 16
NZ = 512


def block_levels(stream_key, shape, cuts, low, high):
    gain, own = 1.0, jax.random.fold_in(stream_key, 6)
    for axis_at, shards_of in cuts:
        steps = jnp.exp(jax.random.uniform(jax.random.fold_in(own, axis_at), (shards_of,), jnp.float32, low / len(cuts), high / len(cuts)))
        gain = gain * jnp.repeat(steps, shape[axis_at] // shards_of).reshape([-1 if axis == axis_at else 1 for axis in range(len(shape))])
    return gain


def noise(stream_key, dims, scale, most, shards=(), kind=jnp.bfloat16):
    level = block_levels(stream_key, dims, shards, -0.22, 0.18) if shards else 1.0
    entries = jax.random.normal(stream_key, dims, jnp.float32) * scale * level
    return jnp.minimum(jnp.maximum(entries, -most), most).astype(kind)


def setup_inputs(seed: int = 0) -> dict:
    keys = jax.random.split(jax.random.key(seed), 4)
    modes = noise(keys[0], (MODES, 3, NZ, EY, EX), 0.05, 0.29882812, ((0, 4), (2, 256)))
    eigenvalues = jnp.clip(jnp.exp(math.log(50.0) - 3.218876 * jax.random.uniform(keys[1], (MODES,), jnp.float32) ** block_levels(keys[1], (MODES,), ((0, 4),), -0.2, 0.2)), 2.0, 50.0)
    density = jnp.clip(0.1 + 0.9 * jax.random.uniform(keys[2], (NZ, EY, EX), jnp.float32) ** block_levels(keys[2], (NZ, EY, EX), ((0, 256),), -0.2, 0.2), 0.1, 1.0)
    return {"modes": modes, "eigenvalues": eigenvalues, "density": density}


def element_tables():
    poisson = 0.3
    lame_first = poisson / ((1.0 + poisson) * (1.0 - 2.0 * poisson))
    shear = 0.5 / (1.0 + poisson)
    elastic = np.zeros((6, 6))
    elastic[:3, :3] = lame_first
    for axis_bit in range(3):
        elastic[axis_bit, axis_bit] += 2.0 * shear
        elastic[axis_bit + 3, axis_bit + 3] = shear
    stiffness = np.zeros((24, 24))
    mass_small = np.zeros((8, 8))
    point = 1.0 / np.sqrt(3.0)
    for gauss in range(8):
        coords = [point * (2 * (gauss >> axis_bit & 1) - 1) for axis_bit in range(3)]
        shape_values = np.zeros(8)
        grads = np.zeros((3, 8))
        for corner in range(8):
            signs = [2 * (corner >> axis_bit & 1) - 1 for axis_bit in range(3)]
            factors = [1.0 + signs[axis_bit] * coords[axis_bit] for axis_bit in range(3)]
            shape_values[corner] = 0.125 * factors[0] * factors[1] * factors[2]
            grads[0, corner] = 0.25 * signs[0] * factors[1] * factors[2]
            grads[1, corner] = 0.25 * signs[1] * factors[0] * factors[2]
            grads[2, corner] = 0.25 * signs[2] * factors[0] * factors[1]
        strain = np.zeros((6, 24))
        for corner in range(8):
            column = 3 * corner
            strain[0, column] = grads[0, corner]
            strain[1, column + 1] = grads[1, corner]
            strain[2, column + 2] = grads[2, corner]
            strain[3, column] = grads[1, corner]
            strain[3, column + 1] = grads[0, corner]
            strain[4, column + 1] = grads[2, corner]
            strain[4, column + 2] = grads[1, corner]
            strain[5, column] = grads[2, corner]
            strain[5, column + 2] = grads[0, corner]
        stiffness = stiffness + strain.T @ elastic @ strain * 0.125
        mass_small = mass_small + np.outer(shape_values, shape_values) * 0.125
    mass = np.kron(mass_small, np.eye(3))
    return np.concatenate([stiffness, mass], 0).astype(np.float32)

def element_forms(field, table):
    depth = field.shape[1] - 1
    height = field.shape[2]
    width = field.shape[3]
    padded = jnp.pad(field, ((0, 0), (0, 0), (0, 1), (0, 1)))
    pieces = []
    for corner in range(8):
        x_off = corner & 1
        y_off = corner >> 1 & 1
        z_off = corner >> 2
        for component in range(3):
            pieces.append(padded[component, z_off:z_off + depth, y_off:y_off + height, x_off:x_off + width].reshape(-1))
    stacked = jnp.stack(pieces)
    images = jnp.dot(table, stacked, preferred_element_type=jnp.float32)
    values = stacked.astype(jnp.float32)
    stiff_form = lax.optimization_barrier(jnp.sum(values * images[:24], 0)).reshape(depth, height, width)
    mass_form = lax.optimization_barrier(jnp.sum(values * images[24:], 0)).reshape(depth, height, width)
    return (stiff_form, mass_form)

def filter_weights():
    listed = []
    for z_step in range(-2, 3):
        for y_step in range(-2, 3):
            for x_step in range(-2, 3):
                weight = 2.5 - float(np.sqrt(z_step * z_step + y_step * y_step + x_step * x_step))
                if weight > 0.0:
                    listed.append((z_step, y_step, x_step, weight))
    return listed

def apply_stencil(padded, weights):
    depth = padded.shape[0] - 4
    height = padded.shape[1] - 4
    width = padded.shape[2] - 4
    total = jnp.zeros((depth, height, width), padded.dtype)
    for z_step, y_step, x_step, weight in weights:
        total = total + weight * padded[2 + z_step:2 + z_step + depth, 2 + y_step:2 + y_step + height, 2 + x_step:2 + x_step + width]
    return total

def reference(modes, eigenvalues, density):
    table = jnp.asarray(element_tables()).astype(jnp.bfloat16)

    def one_mode(carry, inputs):
        field, value = inputs
        field = jnp.pad(field, ((0, 0), (0, 1), (0, 0), (0, 0)))
        stiff_form, mass_form = element_forms(field, table)
        return ((carry[0] + stiff_form, carry[1] + value * mass_form), None)
    zeros = jnp.zeros(density.shape, jnp.float32)
    (stiff_total, mass_total), unused = lax.scan(one_mode, (zeros, zeros), (modes, eigenvalues))
    slope = 3.0 * (1.0 - 0.001) * density * density
    sensitivity = slope * stiff_total - mass_total
    weights = filter_weights()
    totals = apply_stencil(jnp.pad(jnp.ones(density.shape, jnp.float32), 2), weights)
    scaled = sensitivity / totals
    return apply_stencil(jnp.pad(scaled, 2), weights)
```

```python
import functools

import jax
import jax.numpy as jnp
import ml_dtypes
import numpy as np
from jax import lax
from jax.experimental import pallas as pl
from jax.experimental.pallas import tpu as pltpu
from jax.sharding import PartitionSpec as P


def shifted(value, axis, steps):
    count = lax.axis_size(axis)
    first, last = (max(0, -steps), min(count, count - steps))
    return lax.ppermute(value, axis, [(source, source + steps) for source in range(first, last)])


def element_tables():
    poisson = 0.3
    lame_first = poisson / ((1.0 + poisson) * (1.0 - 2.0 * poisson))
    shear = 0.5 / (1.0 + poisson)
    elastic = np.zeros((6, 6))
    elastic[:3, :3] = lame_first
    for axis_bit in range(3):
        elastic[axis_bit, axis_bit] += 2.0 * shear
        elastic[axis_bit + 3, axis_bit + 3] = shear
    stiffness = np.zeros((24, 24))
    mass_small = np.zeros((8, 8))
    point = 1.0 / np.sqrt(3.0)
    for gauss in range(8):
        coords = [point * (2 * (gauss >> axis_bit & 1) - 1) for axis_bit in range(3)]
        shape_values = np.zeros(8)
        grads = np.zeros((3, 8))
        for corner in range(8):
            signs = [2 * (corner >> axis_bit & 1) - 1 for axis_bit in range(3)]
            factors = [1.0 + signs[axis_bit] * coords[axis_bit] for axis_bit in range(3)]
            shape_values[corner] = 0.125 * factors[0] * factors[1] * factors[2]
            grads[0, corner] = 0.25 * signs[0] * factors[1] * factors[2]
            grads[1, corner] = 0.25 * signs[1] * factors[0] * factors[2]
            grads[2, corner] = 0.25 * signs[2] * factors[0] * factors[1]
        strain = np.zeros((6, 24))
        for corner in range(8):
            column = 3 * corner
            strain[0, column] = grads[0, corner]
            strain[1, column + 1] = grads[1, corner]
            strain[2, column + 2] = grads[2, corner]
            strain[3, column] = grads[1, corner]
            strain[3, column + 1] = grads[0, corner]
            strain[4, column + 1] = grads[2, corner]
            strain[4, column + 2] = grads[1, corner]
            strain[5, column] = grads[2, corner]
            strain[5, column + 2] = grads[0, corner]
        stiffness = stiffness + strain.T @ elastic @ strain * 0.125
        mass_small = mass_small + np.outer(shape_values, shape_values) * 0.125
    mass = np.kron(mass_small, np.eye(3))
    return np.concatenate([stiffness, mass], 0).astype(np.float32)


def rounded_tables():
    table = element_tables().astype(ml_dtypes.bfloat16).astype(np.float32)
    return table[:24], table[24:]


def quadratic_form(matrix, u):
    total = None
    for i in range(24):
        term = None
        if matrix[i, i] != 0.0:
            term = float(matrix[i, i]) * u[i]
        row = matrix[i, i + 1 :]
        for value in np.unique(row[row != 0.0]):
            group = None
            for j in np.nonzero(row == value)[0]:
                group = u[i + 1 + j] if group is None else group + u[i + 1 + j]
            piece = float(2.0 * value) * group
            term = piece if term is None else term + piece
        if term is None:
            continue
        piece = u[i] * term
        total = piece if total is None else total + piece
    return total


def filter_offsets():
    listed = []
    for z_step in range(-2, 3):
        for y_step in range(-2, 3):
            for x_step in range(-2, 3):
                weight = 2.5 - float(np.sqrt(z_step * z_step + y_step * y_step + x_step * x_step))
                if weight > 0.0:
                    listed.append((z_step, y_step, x_step, weight))
    return listed


def totals_table(depth, height, width, blocks):
    listed = filter_offsets()
    out = []
    for first_layer in (0, depth, (blocks - 1) * depth):
        total = np.zeros((depth, height, width), np.float64)
        for z in range(depth):
            for z_step, y_step, x_step, weight in listed:
                layer = first_layer + z + z_step
                if layer < 0 or layer >= blocks * depth:
                    continue
                ys = np.arange(height) + y_step
                xs = np.arange(width) + x_step
                inside = ((ys >= 0) & (ys < height))[:, None] & ((xs >= 0) & (xs < width))[None, :]
                total[z] += weight * inside
        out.append(total)
    return np.stack(out).astype(np.float32)


def form_kernel(layer, *refs):
    if layer == 0:
        modes_ref, dens_ref, tot_ref, eig_ref, case_ref, out_ref, sh_ref = refs
        upper_ref = prev_ref = None
    else:
        modes_ref, upper_ref, prev_ref, dens_ref, tot_ref, eig_ref, case_ref, out_ref, sh_ref = refs
    count = modes_ref.shape[0]
    height = modes_ref.shape[3]
    width = modes_ref.shape[4]
    stiff_matrix, mass_matrix = rounded_tables()
    lane = lax.broadcasted_iota(jnp.int32, (height, width), 1)
    row = lax.broadcasted_iota(jnp.int32, (height, width), 0)
    x_edge = lane == width - 1
    y_edge = row == height - 1

    def plane(m, k, p):
        if layer == 0 or p == 0:
            return modes_ref[m, k, layer + p].astype(jnp.float32)
        return upper_ref[m, k, 0].astype(jnp.float32)

    def prepare(m, carry):
        for k in range(3):
            for p in range(2):
                base = plane(m, k, p)
                along_x = jnp.where(x_edge, 0.0, pltpu.roll(base, width - 1, 1))
                along_y = jnp.where(y_edge, 0.0, pltpu.roll(base, height - 1, 0))
                along_xy = jnp.where(y_edge, 0.0, pltpu.roll(along_x, height - 1, 0))
                sh_ref[m, k, p, 0] = base
                sh_ref[m, k, p, 1] = along_x
                sh_ref[m, k, p, 2] = along_y
                sh_ref[m, k, p, 3] = along_xy
        return carry

    lax.fori_loop(0, count, prepare, 0)

    chunks = height // 8

    def accumulate(m, carry):
        value = eig_ref[m]
        new = []
        for b in range(chunks):
            rows = slice(8 * b, 8 * b + 8)
            u = []
            for corner in range(8):
                x_off = corner & 1
                y_off = corner >> 1 & 1
                z_off = corner >> 2
                for k in range(3):
                    u.append(sh_ref[m, k, z_off, x_off + 2 * y_off, rows, :])
            stiff = quadratic_form(stiff_matrix, u)
            mass = quadratic_form(mass_matrix, u)
            new.append(carry[2 * b] + stiff)
            new.append(carry[2 * b + 1] + value * mass)
        return tuple(new)

    zero = jnp.zeros((8, width), jnp.float32)
    sums = lax.fori_loop(0, count, accumulate, tuple(zero for _ in range(2 * chunks)))
    case = case_ref[0]
    if layer == 1:
        out_ref[0] = prev_ref[0]
    for b in range(chunks):
        rows = slice(8 * b, 8 * b + 8)
        density = dens_ref[layer, rows, :]
        slope = 3.0 * (1.0 - 0.001) * density * density
        sensitivity = slope * sums[2 * b] - sums[2 * b + 1]
        out_ref[layer, rows, :] = sensitivity / tot_ref[case, layer, rows, :]


def element_pass(layer, operands, depth, height, width, count):
    vmem = pl.BlockSpec(memory_space=pltpu.VMEM)
    smem = pl.BlockSpec(memory_space=pltpu.SMEM)
    specs = [vmem] * (len(operands) - 2) + [smem, smem]
    return pl.pallas_call(
        functools.partial(form_kernel, layer),
        out_shape=jax.ShapeDtypeStruct((depth, height, width), jnp.float32),
        in_specs=specs,
        out_specs=vmem,
        scratch_shapes=[pltpu.VMEM((count, 3, 2, 4, height, width), jnp.float32)],
    )(*operands)


def stencil_bands(width):
    offsets = []
    bands = []
    for z_step in range(-2, 3):
        for y_step in range(-2, 3):
            band = np.zeros((width, width), np.float32)
            used = False
            for x_step in range(-2, 3):
                weight = 2.5 - float(np.sqrt(z_step * z_step + y_step * y_step + x_step * x_step))
                if weight > 0.0:
                    band = band + weight * np.eye(width, k=-x_step, dtype=np.float32)
                    used = True
            if used:
                offsets.append((z_step, y_step))
                bands.append(band)
    return (offsets, np.stack(bands))


def apply_stencil(padded, width):
    depth = padded.shape[0] - 4
    height = padded.shape[1] - 4
    offsets, bands = stencil_bands(width)
    stacked = jnp.stack(
        [
            padded[2 + z_step : 2 + z_step + depth, 2 + y_step : 2 + y_step + height, :]
            for z_step, y_step in offsets
        ]
    )
    return jnp.einsum(
        "kzyx,kxw->zyw",
        stacked,
        jnp.asarray(bands),
        precision=lax.Precision.HIGHEST,
        preferred_element_type=jnp.float32,
    )


def local(modes, eigenvalues, density):
    count = modes.shape[0]
    depth = density.shape[0]
    height = density.shape[1]
    width = density.shape[2]
    blocks = lax.axis_size("grid")
    g = lax.axis_index("grid")
    case = ((g > 0).astype(jnp.int32) + (g == blocks - 1).astype(jnp.int32)).reshape(1)
    totals = jnp.asarray(totals_table(depth, height, width, blocks))
    upper = shifted(modes[:, :, :1], "grid", -1)
    first = element_pass(0, (modes, density, totals, eigenvalues, case), depth, height, width, count)
    scaled = element_pass(
        1, (modes, upper, first, density, totals, eigenvalues, case), depth, height, width, count
    )
    modes_count = lax.axis_size("mode")
    got = [lax.ppermute(scaled, "mode", [(m, m ^ s) for m in range(modes_count)]) for s in (1, 2, 3)]
    block = (scaled + got[0]) + (got[1] + got[2])
    low = shifted(block, "grid", 1)
    high = shifted(block, "grid", -1)
    widened = jnp.concatenate([low, block, high], 0)
    widened = jnp.pad(widened, ((0, 0), (2, 2), (0, 0)))
    return apply_stencil(widened, width)


def solution(mesh):
    in_specs = (P("mode", None, "grid", None, None), P("mode"), P("grid", None, None))
    out_specs = P("grid", None, None)
    return jax.shard_map(local, mesh=mesh, in_specs=in_specs, out_specs=out_specs, check_vma=False)
```

```python
import functools

import jax
import jax.numpy as jnp
import ml_dtypes
import numpy as np
from jax import lax
from jax.experimental import pallas as pl
from jax.experimental.pallas import tpu as pltpu
from jax.sharding import PartitionSpec as P


def shifted(value, axis, steps):
    count = lax.axis_size(axis)
    first, last = (max(0, -steps), min(count, count - steps))
    return lax.ppermute(value, axis, [(source, source + steps) for source in range(first, last)])


def element_tables():
    poisson = 0.3
    lame_first = poisson / ((1.0 + poisson) * (1.0 - 2.0 * poisson))
    shear = 0.5 / (1.0 + poisson)
    elastic = np.zeros((6, 6))
    elastic[:3, :3] = lame_first
    for axis_bit in range(3):
        elastic[axis_bit, axis_bit] += 2.0 * shear
        elastic[axis_bit + 3, axis_bit + 3] = shear
    stiffness = np.zeros((24, 24))
    mass_small = np.zeros((8, 8))
    point = 1.0 / np.sqrt(3.0)
    for gauss in range(8):
        coords = [point * (2 * (gauss >> axis_bit & 1) - 1) for axis_bit in range(3)]
        shape_values = np.zeros(8)
        grads = np.zeros((3, 8))
        for corner in range(8):
            signs = [2 * (corner >> axis_bit & 1) - 1 for axis_bit in range(3)]
            factors = [1.0 + signs[axis_bit] * coords[axis_bit] for axis_bit in range(3)]
            shape_values[corner] = 0.125 * factors[0] * factors[1] * factors[2]
            grads[0, corner] = 0.25 * signs[0] * factors[1] * factors[2]
            grads[1, corner] = 0.25 * signs[1] * factors[0] * factors[2]
            grads[2, corner] = 0.25 * signs[2] * factors[0] * factors[1]
        strain = np.zeros((6, 24))
        for corner in range(8):
            column = 3 * corner
            strain[0, column] = grads[0, corner]
            strain[1, column + 1] = grads[1, corner]
            strain[2, column + 2] = grads[2, corner]
            strain[3, column] = grads[1, corner]
            strain[3, column + 1] = grads[0, corner]
            strain[4, column + 1] = grads[2, corner]
            strain[4, column + 2] = grads[1, corner]
            strain[5, column] = grads[2, corner]
            strain[5, column + 2] = grads[0, corner]
        stiffness = stiffness + strain.T @ elastic @ strain * 0.125
        mass_small = mass_small + np.outer(shape_values, shape_values) * 0.125
    mass = np.kron(mass_small, np.eye(3))
    return np.concatenate([stiffness, mass], 0).astype(np.float32)


def rounded_tables():
    table = element_tables().astype(ml_dtypes.bfloat16).astype(np.float32)
    return table[:24], table[24:]


def quadratic_form(matrix, u):
    total = None
    for i in range(24):
        term = None
        if matrix[i, i] != 0.0:
            term = float(matrix[i, i]) * u[i]
        row = matrix[i, i + 1 :]
        for value in np.unique(row[row != 0.0]):
            group = None
            for j in np.nonzero(row == value)[0]:
                group = u[i + 1 + j] if group is None else group + u[i + 1 + j]
            piece = float(2.0 * value) * group
            term = piece if term is None else term + piece
        if term is None:
            continue
        piece = u[i] * term
        total = piece if total is None else total + piece
    return total


def filter_offsets():
    listed = []
    for z_step in range(-2, 3):
        for y_step in range(-2, 3):
            for x_step in range(-2, 3):
                weight = 2.5 - float(np.sqrt(z_step * z_step + y_step * y_step + x_step * x_step))
                if weight > 0.0:
                    listed.append((z_step, y_step, x_step, weight))
    return listed


def totals_table(depth, height, width, blocks):
    listed = filter_offsets()
    out = []
    for first_layer in (0, depth, (blocks - 1) * depth):
        total = np.zeros((depth, height, width), np.float64)
        for z in range(depth):
            for z_step, y_step, x_step, weight in listed:
                layer = first_layer + z + z_step
                if layer < 0 or layer >= blocks * depth:
                    continue
                ys = np.arange(height) + y_step
                xs = np.arange(width) + x_step
                inside = ((ys >= 0) & (ys < height))[:, None] & ((xs >= 0) & (xs < width))[None, :]
                total[z] += weight * inside
        out.append(total)
    return np.stack(out).astype(np.float32)


def form_kernel(layer, *refs):
    if layer == 0:
        modes_ref, dens_ref, tot_ref, eig_ref, case_ref, out_ref, sh_ref = refs
        upper_ref = prev_ref = None
    else:
        modes_ref, upper_ref, prev_ref, dens_ref, tot_ref, eig_ref, case_ref, out_ref, sh_ref = refs
    count = modes_ref.shape[0]
    height = modes_ref.shape[3]
    width = modes_ref.shape[4]
    stiff_matrix, mass_matrix = rounded_tables()
    lane = lax.broadcasted_iota(jnp.int32, (height, width), 1)
    row = lax.broadcasted_iota(jnp.int32, (height, width), 0)
    x_edge = lane == width - 1
    y_edge = row == height - 1

    def plane(m, k, p):
        if layer == 0 or p == 0:
            return modes_ref[m, k, layer + p].astype(jnp.float32)
        return upper_ref[m, k, 0].astype(jnp.float32)

    def prepare(m, carry):
        for k in range(3):
            for p in range(2):
                base = plane(m, k, p)
                along_x = jnp.where(x_edge, 0.0, pltpu.roll(base, width - 1, 1))
                along_y = jnp.where(y_edge, 0.0, pltpu.roll(base, height - 1, 0))
                along_xy = jnp.where(y_edge, 0.0, pltpu.roll(along_x, height - 1, 0))
                sh_ref[m, k, p, 0] = base
                sh_ref[m, k, p, 1] = along_x
                sh_ref[m, k, p, 2] = along_y
                sh_ref[m, k, p, 3] = along_xy
        return carry

    lax.fori_loop(0, count, prepare, 0)

    chunks = height // 8

    def accumulate(m, carry):
        value = eig_ref[m]
        new = []
        for b in range(chunks):
            rows = slice(8 * b, 8 * b + 8)
            u = []
            for corner in range(8):
                x_off = corner & 1
                y_off = corner >> 1 & 1
                z_off = corner >> 2
                for k in range(3):
                    u.append(sh_ref[m, k, z_off, x_off + 2 * y_off, rows, :])
            stiff = quadratic_form(stiff_matrix, u)
            mass = quadratic_form(mass_matrix, u)
            new.append(carry[2 * b] + stiff)
            new.append(carry[2 * b + 1] + value * mass)
        return tuple(new)

    zero = jnp.zeros((8, width), jnp.float32)
    sums = lax.fori_loop(0, count, accumulate, tuple(zero for _ in range(2 * chunks)))
    case = case_ref[0]
    if layer == 1:
        out_ref[0] = prev_ref[0]
    for b in range(chunks):
        rows = slice(8 * b, 8 * b + 8)
        density = dens_ref[layer, rows, :]
        slope = 3.0 * (1.0 - 0.001) * density * density
        sensitivity = slope * sums[2 * b] - sums[2 * b + 1]
        out_ref[layer, rows, :] = sensitivity / tot_ref[case, layer, rows, :]


def element_pass(layer, operands, depth, height, width, count):
    vmem = pl.BlockSpec(memory_space=pltpu.VMEM)
    smem = pl.BlockSpec(memory_space=pltpu.SMEM)
    specs = [vmem] * (len(operands) - 2) + [smem, smem]
    return pl.pallas_call(
        functools.partial(form_kernel, layer),
        out_shape=jax.ShapeDtypeStruct((depth, height, width), jnp.float32),
        in_specs=specs,
        out_specs=vmem,
        scratch_shapes=[pltpu.VMEM((count, 3, 2, 4, height, width), jnp.float32)],
    )(*operands)


def stencil_bands(width):
    offsets = []
    bands = []
    for z_step in range(-2, 3):
        for y_step in range(-2, 3):
            band = np.zeros((width, width), np.float32)
            used = False
            for x_step in range(-2, 3):
                weight = 2.5 - float(np.sqrt(z_step * z_step + y_step * y_step + x_step * x_step))
                if weight > 0.0:
                    band = band + weight * np.eye(width, k=-x_step, dtype=np.float32)
                    used = True
            if used:
                offsets.append((z_step, y_step))
                bands.append(band)
    return (offsets, np.stack(bands))


def apply_stencil(padded, width):
    depth = padded.shape[0] - 4
    height = padded.shape[1] - 4
    offsets, bands = stencil_bands(width)
    stacked = jnp.stack(
        [
            padded[2 + z_step : 2 + z_step + depth, 2 + y_step : 2 + y_step + height, :]
            for z_step, y_step in offsets
        ]
    )
    return jnp.einsum(
        "kzyx,kxw->zyw",
        stacked,
        jnp.asarray(bands),
        precision=lax.Precision.HIGHEST,
        preferred_element_type=jnp.float32,
    )


def local(modes, eigenvalues, density):
    count = modes.shape[0]
    depth = density.shape[0]
    height = density.shape[1]
    width = density.shape[2]
    blocks = lax.axis_size("grid")
    g = lax.axis_index("grid")
    case = ((g > 0).astype(jnp.int32) + (g == blocks - 1).astype(jnp.int32)).reshape(1)
    totals = jnp.asarray(totals_table(depth, height, width, blocks))
    upper = shifted(modes[:, :, :1], "grid", -1)
    first = element_pass(0, (modes, density, totals, eigenvalues, case), depth, height, width, count)
    scaled = element_pass(
        1, (modes, upper, first, density, totals, eigenvalues, case), depth, height, width, count
    )
    modes_count = lax.axis_size("mode")
    sent = scaled.astype(jnp.bfloat16)
    got = [lax.ppermute(sent, "mode", [(m, m ^ s) for m in range(modes_count)]) for s in (1, 2, 3)]
    got = [part.astype(jnp.float32) for part in got]
    block = (sent.astype(jnp.float32) + got[0]) + (got[1] + got[2])
    halo = block.astype(jnp.bfloat16)
    low = shifted(halo, "grid", 1).astype(jnp.float32)
    high = shifted(halo, "grid", -1).astype(jnp.float32)
    widened = jnp.concatenate([low, block, high], 0)
    widened = jnp.pad(widened, ((0, 0), (2, 2), (0, 0)))
    return apply_stencil(widened, width)


def solution(mesh):
    in_specs = (P("mode", None, "grid", None, None), P("mode"), P("grid", None, None))
    out_specs = P("grid", None, None)
    return jax.shard_map(local, mesh=mesh, in_specs=in_specs, out_specs=out_specs, check_vma=False)
```

```python
import functools

import jax
import jax.numpy as jnp
import ml_dtypes
import numpy as np
from jax import lax
from jax.experimental import pallas as pl
from jax.experimental.pallas import tpu as pltpu
from jax.sharding import PartitionSpec as P


def shifted(value, axis, steps):
    count = lax.axis_size(axis)
    first, last = (max(0, -steps), min(count, count - steps))
    return lax.ppermute(value, axis, [(source, source + steps) for source in range(first, last)])


def element_tables():
    poisson = 0.3
    lame_first = poisson / ((1.0 + poisson) * (1.0 - 2.0 * poisson))
    shear = 0.5 / (1.0 + poisson)
    elastic = np.zeros((6, 6))
    elastic[:3, :3] = lame_first
    for axis_bit in range(3):
        elastic[axis_bit, axis_bit] += 2.0 * shear
        elastic[axis_bit + 3, axis_bit + 3] = shear
    stiffness = np.zeros((24, 24))
    mass_small = np.zeros((8, 8))
    point = 1.0 / np.sqrt(3.0)
    for gauss in range(8):
        coords = [point * (2 * (gauss >> axis_bit & 1) - 1) for axis_bit in range(3)]
        shape_values = np.zeros(8)
        grads = np.zeros((3, 8))
        for corner in range(8):
            signs = [2 * (corner >> axis_bit & 1) - 1 for axis_bit in range(3)]
            factors = [1.0 + signs[axis_bit] * coords[axis_bit] for axis_bit in range(3)]
            shape_values[corner] = 0.125 * factors[0] * factors[1] * factors[2]
            grads[0, corner] = 0.25 * signs[0] * factors[1] * factors[2]
            grads[1, corner] = 0.25 * signs[1] * factors[0] * factors[2]
            grads[2, corner] = 0.25 * signs[2] * factors[0] * factors[1]
        strain = np.zeros((6, 24))
        for corner in range(8):
            column = 3 * corner
            strain[0, column] = grads[0, corner]
            strain[1, column + 1] = grads[1, corner]
            strain[2, column + 2] = grads[2, corner]
            strain[3, column] = grads[1, corner]
            strain[3, column + 1] = grads[0, corner]
            strain[4, column + 1] = grads[2, corner]
            strain[4, column + 2] = grads[1, corner]
            strain[5, column] = grads[2, corner]
            strain[5, column + 2] = grads[0, corner]
        stiffness = stiffness + strain.T @ elastic @ strain * 0.125
        mass_small = mass_small + np.outer(shape_values, shape_values) * 0.125
    mass = np.kron(mass_small, np.eye(3))
    return np.concatenate([stiffness, mass], 0).astype(np.float32)


def rounded_tables():
    table = element_tables().astype(ml_dtypes.bfloat16).astype(np.float32)
    return table[:24], table[24:]


def quadratic_form(matrix, u):
    total = None
    for i in range(24):
        term = None
        if matrix[i, i] != 0.0:
            term = float(matrix[i, i]) * u[i]
        row = matrix[i, i + 1 :]
        for value in np.unique(row[row != 0.0]):
            group = None
            for j in np.nonzero(row == value)[0]:
                group = u[i + 1 + j] if group is None else group + u[i + 1 + j]
            piece = float(2.0 * value) * group
            term = piece if term is None else term + piece
        if term is None:
            continue
        piece = u[i] * term
        total = piece if total is None else total + piece
    return total


def filter_offsets():
    listed = []
    for z_step in range(-2, 3):
        for y_step in range(-2, 3):
            for x_step in range(-2, 3):
                weight = 2.5 - float(np.sqrt(z_step * z_step + y_step * y_step + x_step * x_step))
                if weight > 0.0:
                    listed.append((z_step, y_step, x_step, weight))
    return listed


def totals_table(depth, height, width, blocks):
    listed = filter_offsets()
    out = []
    for first_layer in (0, depth, (blocks - 1) * depth):
        total = np.zeros((depth, height, width), np.float64)
        for z in range(depth):
            for z_step, y_step, x_step, weight in listed:
                layer = first_layer + z + z_step
                if layer < 0 or layer >= blocks * depth:
                    continue
                ys = np.arange(height) + y_step
                xs = np.arange(width) + x_step
                inside = ((ys >= 0) & (ys < height))[:, None] & ((xs >= 0) & (xs < width))[None, :]
                total[z] += weight * inside
        out.append(total)
    return np.stack(out).astype(np.float32)


def form_kernel(layer, *refs):
    if layer == 0:
        modes_ref, dens_ref, tot_ref, eig_ref, case_ref, out_ref, sh_ref = refs
        upper_ref = prev_ref = None
    else:
        modes_ref, upper_ref, prev_ref, dens_ref, tot_ref, eig_ref, case_ref, out_ref, sh_ref = refs
    count = modes_ref.shape[0]
    height = modes_ref.shape[3]
    width = modes_ref.shape[4]
    stiff_matrix, mass_matrix = rounded_tables()
    lane = lax.broadcasted_iota(jnp.int32, (height, width), 1)
    row = lax.broadcasted_iota(jnp.int32, (height, width), 0)
    x_edge = lane == width - 1
    y_edge = row == height - 1

    def plane(m, k, p):
        if layer == 0 or p == 0:
            return modes_ref[m, k, layer + p].astype(jnp.float32)
        return upper_ref[m, k, 0].astype(jnp.float32)

    def prepare(m, carry):
        for k in range(3):
            for p in range(2):
                base = plane(m, k, p)
                along_x = jnp.where(x_edge, 0.0, pltpu.roll(base, width - 1, 1))
                along_y = jnp.where(y_edge, 0.0, pltpu.roll(base, height - 1, 0))
                along_xy = jnp.where(y_edge, 0.0, pltpu.roll(along_x, height - 1, 0))
                sh_ref[m, k, p, 0] = base
                sh_ref[m, k, p, 1] = along_x
                sh_ref[m, k, p, 2] = along_y
                sh_ref[m, k, p, 3] = along_xy
        return carry

    lax.fori_loop(0, count, prepare, 0)

    chunks = height // 8

    def accumulate(m, carry):
        value = eig_ref[m]
        new = []
        for b in range(chunks):
            rows = slice(8 * b, 8 * b + 8)
            u = []
            for corner in range(8):
                x_off = corner & 1
                y_off = corner >> 1 & 1
                z_off = corner >> 2
                for k in range(3):
                    u.append(sh_ref[m, k, z_off, x_off + 2 * y_off, rows, :])
            stiff = quadratic_form(stiff_matrix, u)
            mass = quadratic_form(mass_matrix, u)
            new.append(carry[2 * b] + stiff)
            new.append(carry[2 * b + 1] + value * mass)
        return tuple(new)

    zero = jnp.zeros((8, width), jnp.float32)
    sums = lax.fori_loop(0, count, accumulate, tuple(zero for _ in range(2 * chunks)))
    case = case_ref[0]
    if layer == 1:
        out_ref[0] = prev_ref[0]
    for b in range(chunks):
        rows = slice(8 * b, 8 * b + 8)
        density = dens_ref[layer, rows, :]
        slope = 3.0 * (1.0 - 0.001) * density * density
        sensitivity = slope * sums[2 * b] - sums[2 * b + 1]
        out_ref[layer, rows, :] = sensitivity / tot_ref[case, layer, rows, :]


def element_pass(layer, operands, depth, height, width, count):
    vmem = pl.BlockSpec(memory_space=pltpu.VMEM)
    smem = pl.BlockSpec(memory_space=pltpu.SMEM)
    specs = [vmem] * (len(operands) - 2) + [smem, smem]
    return pl.pallas_call(
        functools.partial(form_kernel, layer),
        out_shape=jax.ShapeDtypeStruct((depth, height, width), jnp.float32),
        in_specs=specs,
        out_specs=vmem,
        scratch_shapes=[pltpu.VMEM((count, 3, 2, 4, height, width), jnp.float32)],
    )(*operands)


def stencil_bands(width):
    offsets = []
    bands = []
    for z_step in range(-2, 3):
        for y_step in range(-2, 3):
            band = np.zeros((width, width), np.float32)
            used = False
            for x_step in range(-2, 3):
                weight = 2.5 - float(np.sqrt(z_step * z_step + y_step * y_step + x_step * x_step))
                if weight > 0.0:
                    band = band + weight * np.eye(width, k=-x_step, dtype=np.float32)
                    used = True
            if used:
                offsets.append((z_step, y_step))
                bands.append(band)
    return (offsets, np.stack(bands))


def apply_stencil(padded, width):
    depth = padded.shape[0] - 4
    height = padded.shape[1] - 4
    offsets, bands = stencil_bands(width)
    stacked = jnp.stack(
        [
            padded[2 + z_step : 2 + z_step + depth, 2 + y_step : 2 + y_step + height, :]
            for z_step, y_step in offsets
        ]
    )
    return jnp.einsum(
        "kzyx,kxw->zyw",
        stacked,
        jnp.asarray(bands),
        precision=lax.Precision.HIGHEST,
        preferred_element_type=jnp.float32,
    )


def local(modes, eigenvalues, density):
    count = modes.shape[0]
    depth = density.shape[0]
    height = density.shape[1]
    width = density.shape[2]
    blocks = lax.axis_size("grid")
    g = lax.axis_index("grid")
    case = ((g > 0).astype(jnp.int32) + (g == blocks - 1).astype(jnp.int32)).reshape(1)
    totals = jnp.asarray(totals_table(depth, height, width, blocks))
    upper = shifted(modes[:, :, :1], "grid", -1)
    first = element_pass(0, (modes, density, totals, eigenvalues, case), depth, height, width, count)
    scaled = element_pass(
        1, (modes, upper, first, density, totals, eigenvalues, case), depth, height, width, count
    )
    modes_count = lax.axis_size("mode")
    sent = scaled.astype(jnp.bfloat16)
    spread = jnp.broadcast_to(sent[None], (modes_count,) + sent.shape)
    got = lax.all_to_all(spread, "mode", 0, 0, tiled=False).astype(jnp.float32)
    block = (got[0] + got[1]) + (got[2] + got[3])
    halo = block.astype(jnp.bfloat16)
    low = shifted(halo, "grid", 1).astype(jnp.float32)
    high = shifted(halo, "grid", -1).astype(jnp.float32)
    widened = jnp.concatenate([low, block, high], 0)
    widened = jnp.pad(widened, ((0, 0), (2, 2), (0, 0)))
    return apply_stencil(widened, width)


def solution(mesh):
    in_specs = (P("mode", None, "grid", None, None), P("mode"), P("grid", None, None))
    out_specs = P("grid", None, None)
    return jax.shard_map(local, mesh=mesh, in_specs=in_specs, out_specs=out_specs, check_vma=False)
```

```python
import functools

import jax
import jax.numpy as jnp
import ml_dtypes
import numpy as np
from jax import lax
from jax.experimental import pallas as pl
from jax.experimental.pallas import tpu as pltpu
from jax.sharding import PartitionSpec as P


def shifted(value, axis, steps):
    count = lax.axis_size(axis)
    first, last = (max(0, -steps), min(count, count - steps))
    return lax.ppermute(value, axis, [(source, source + steps) for source in range(first, last)])


def element_tables():
    poisson = 0.3
    lame_first = poisson / ((1.0 + poisson) * (1.0 - 2.0 * poisson))
    shear = 0.5 / (1.0 + poisson)
    elastic = np.zeros((6, 6))
    elastic[:3, :3] = lame_first
    for axis_bit in range(3):
        elastic[axis_bit, axis_bit] += 2.0 * shear
        elastic[axis_bit + 3, axis_bit + 3] = shear
    stiffness = np.zeros((24, 24))
    mass_small = np.zeros((8, 8))
    point = 1.0 / np.sqrt(3.0)
    for gauss in range(8):
        coords = [point * (2 * (gauss >> axis_bit & 1) - 1) for axis_bit in range(3)]
        shape_values = np.zeros(8)
        grads = np.zeros((3, 8))
        for corner in range(8):
            signs = [2 * (corner >> axis_bit & 1) - 1 for axis_bit in range(3)]
            factors = [1.0 + signs[axis_bit] * coords[axis_bit] for axis_bit in range(3)]
            shape_values[corner] = 0.125 * factors[0] * factors[1] * factors[2]
            grads[0, corner] = 0.25 * signs[0] * factors[1] * factors[2]
            grads[1, corner] = 0.25 * signs[1] * factors[0] * factors[2]
            grads[2, corner] = 0.25 * signs[2] * factors[0] * factors[1]
        strain = np.zeros((6, 24))
        for corner in range(8):
            column = 3 * corner
            strain[0, column] = grads[0, corner]
            strain[1, column + 1] = grads[1, corner]
            strain[2, column + 2] = grads[2, corner]
            strain[3, column] = grads[1, corner]
            strain[3, column + 1] = grads[0, corner]
            strain[4, column + 1] = grads[2, corner]
            strain[4, column + 2] = grads[1, corner]
            strain[5, column] = grads[2, corner]
            strain[5, column + 2] = grads[0, corner]
        stiffness = stiffness + strain.T @ elastic @ strain * 0.125
        mass_small = mass_small + np.outer(shape_values, shape_values) * 0.125
    mass = np.kron(mass_small, np.eye(3))
    return np.concatenate([stiffness, mass], 0).astype(np.float32)


def rounded_tables():
    table = element_tables().astype(ml_dtypes.bfloat16).astype(np.float32)
    return table[:24], table[24:]


def quadratic_form(matrix, u):
    total = None
    for i in range(24):
        term = None
        if matrix[i, i] != 0.0:
            term = float(matrix[i, i]) * u[i]
        row = matrix[i, i + 1 :]
        for value in np.unique(row[row != 0.0]):
            group = None
            for j in np.nonzero(row == value)[0]:
                group = u[i + 1 + j] if group is None else group + u[i + 1 + j]
            piece = float(2.0 * value) * group
            term = piece if term is None else term + piece
        if term is None:
            continue
        piece = u[i] * term
        total = piece if total is None else total + piece
    return total


def filter_offsets():
    listed = []
    for z_step in range(-2, 3):
        for y_step in range(-2, 3):
            for x_step in range(-2, 3):
                weight = 2.5 - float(np.sqrt(z_step * z_step + y_step * y_step + x_step * x_step))
                if weight > 0.0:
                    listed.append((z_step, y_step, x_step, weight))
    return listed


def totals_table(depth, height, width, blocks):
    listed = filter_offsets()
    out = []
    for first_layer in (0, depth, (blocks - 1) * depth):
        total = np.zeros((depth, height, width), np.float64)
        for z in range(depth):
            for z_step, y_step, x_step, weight in listed:
                layer = first_layer + z + z_step
                if layer < 0 or layer >= blocks * depth:
                    continue
                ys = np.arange(height) + y_step
                xs = np.arange(width) + x_step
                inside = ((ys >= 0) & (ys < height))[:, None] & ((xs >= 0) & (xs < width))[None, :]
                total[z] += weight * inside
        out.append(total)
    return np.stack(out).astype(np.float32)


def form_kernel(modes_ref, upper_ref, dens_ref, tot_ref, eig_ref, case_ref, out_ref, sh_ref):
    count = modes_ref.shape[0]
    depth = modes_ref.shape[2]
    height = modes_ref.shape[3]
    width = modes_ref.shape[4]
    stiff_matrix, mass_matrix = rounded_tables()
    lane = lax.broadcasted_iota(jnp.int32, (height, width), 1)
    row = lax.broadcasted_iota(jnp.int32, (height, width), 0)
    x_edge = lane == width - 1
    y_edge = row == height - 1

    def plane(m, k, p):
        if p < depth:
            return modes_ref[m, k, p].astype(jnp.float32)
        return upper_ref[m, k, 0].astype(jnp.float32)

    def prepare(m, carry):
        for k in range(3):
            for p in range(depth + 1):
                base = plane(m, k, p)
                along_x = jnp.where(x_edge, 0.0, pltpu.roll(base, width - 1, 1))
                along_y = jnp.where(y_edge, 0.0, pltpu.roll(base, height - 1, 0))
                along_xy = jnp.where(y_edge, 0.0, pltpu.roll(along_x, height - 1, 0))
                sh_ref[m, k, p, 0] = base
                sh_ref[m, k, p, 1] = along_x
                sh_ref[m, k, p, 2] = along_y
                sh_ref[m, k, p, 3] = along_xy
        return carry

    lax.fori_loop(0, count, prepare, 0)

    chunks = height // 8

    def accumulate(m, carry):
        value = eig_ref[m]
        new = []
        for layer in range(depth):
            for b in range(chunks):
                rows = slice(8 * b, 8 * b + 8)
                u = []
                for corner in range(8):
                    x_off = corner & 1
                    y_off = corner >> 1 & 1
                    z_off = corner >> 2
                    for k in range(3):
                        u.append(sh_ref[m, k, layer + z_off, x_off + 2 * y_off, rows, :])
                stiff = quadratic_form(stiff_matrix, u)
                mass = quadratic_form(mass_matrix, u)
                at = 2 * (layer * chunks + b)
                new.append(carry[at] + stiff)
                new.append(carry[at + 1] + value * mass)
        return tuple(new)

    zero = jnp.zeros((8, width), jnp.float32)
    sums = lax.fori_loop(0, count, accumulate, tuple(zero for _ in range(2 * depth * chunks)))
    case = case_ref[0]
    for layer in range(depth):
        for b in range(chunks):
            rows = slice(8 * b, 8 * b + 8)
            at = 2 * (layer * chunks + b)
            density = dens_ref[layer, rows, :]
            slope = 3.0 * (1.0 - 0.001) * density * density
            sensitivity = slope * sums[at] - sums[at + 1]
            scaled = sensitivity / tot_ref[case, layer, rows, :]
            out_ref[layer, rows, :] = scaled.astype(out_ref.dtype)


def element_pass(operands, depth, height, width, count):
    vmem = pl.BlockSpec(memory_space=pltpu.VMEM)
    smem = pl.BlockSpec(memory_space=pltpu.SMEM)
    specs = [vmem] * (len(operands) - 2) + [smem, smem]
    return pl.pallas_call(
        form_kernel,
        out_shape=jax.ShapeDtypeStruct((depth, height, width), jnp.bfloat16),
        in_specs=specs,
        out_specs=vmem,
        scratch_shapes=[pltpu.VMEM((count, 3, depth + 1, 4, height, width), jnp.float32)],
    )(*operands)


def stencil_bands(width):
    offsets = []
    bands = []
    for z_step in range(-2, 3):
        for y_step in range(-2, 3):
            band = np.zeros((width, width), np.float32)
            used = False
            for x_step in range(-2, 3):
                weight = 2.5 - float(np.sqrt(z_step * z_step + y_step * y_step + x_step * x_step))
                if weight > 0.0:
                    band = band + weight * np.eye(width, k=-x_step, dtype=np.float32)
                    used = True
            if used:
                offsets.append((z_step, y_step))
                bands.append(band)
    return (offsets, np.stack(bands))


def apply_stencil(padded, width):
    depth = padded.shape[0] - 4
    height = padded.shape[1] - 4
    offsets, bands = stencil_bands(width)
    stacked = jnp.stack(
        [
            padded[2 + z_step : 2 + z_step + depth, 2 + y_step : 2 + y_step + height, :]
            for z_step, y_step in offsets
        ]
    )
    return jnp.einsum(
        "kzyx,kxw->zyw",
        stacked,
        jnp.asarray(bands),
        precision=lax.Precision.HIGHEST,
        preferred_element_type=jnp.float32,
    )


def local(modes, eigenvalues, density):
    count = modes.shape[0]
    depth = density.shape[0]
    height = density.shape[1]
    width = density.shape[2]
    blocks = lax.axis_size("grid")
    g = lax.axis_index("grid")
    case = ((g > 0).astype(jnp.int32) + (g == blocks - 1).astype(jnp.int32)).reshape(1)
    totals = jnp.asarray(totals_table(depth, height, width, blocks))
    upper = shifted(modes[:, :, :1], "grid", -1)
    sent = element_pass((modes, upper, density, totals, eigenvalues, case), depth, height, width, count)
    modes_count = lax.axis_size("mode")
    spread = jnp.broadcast_to(sent[None], (modes_count,) + sent.shape)
    got = lax.all_to_all(spread, "mode", 0, 0, tiled=False).astype(jnp.float32)
    block = (got[0] + got[1]) + (got[2] + got[3])
    halo = block.astype(jnp.bfloat16)
    low = shifted(halo, "grid", 1).astype(jnp.float32)
    high = shifted(halo, "grid", -1).astype(jnp.float32)
    widened = jnp.concatenate([low, block, high], 0)
    widened = jnp.pad(widened, ((0, 0), (2, 2), (0, 0)))
    return apply_stencil(widened, width)


def solution(mesh):
    in_specs = (P("mode", None, "grid", None, None), P("mode"), P("grid", None, None))
    out_specs = P("grid", None, None)
    return jax.shard_map(local, mesh=mesh, in_specs=in_specs, out_specs=out_specs, check_vma=False)
```

```python
import functools

import jax
import jax.numpy as jnp
import ml_dtypes
import numpy as np
from jax import lax
from jax.experimental import pallas as pl
from jax.experimental.pallas import tpu as pltpu
from jax.sharding import PartitionSpec as P


def shifted(value, axis, steps):
    count = lax.axis_size(axis)
    first, last = (max(0, -steps), min(count, count - steps))
    return lax.ppermute(value, axis, [(source, source + steps) for source in range(first, last)])


def element_tables():
    poisson = 0.3
    lame_first = poisson / ((1.0 + poisson) * (1.0 - 2.0 * poisson))
    shear = 0.5 / (1.0 + poisson)
    elastic = np.zeros((6, 6))
    elastic[:3, :3] = lame_first
    for axis_bit in range(3):
        elastic[axis_bit, axis_bit] += 2.0 * shear
        elastic[axis_bit + 3, axis_bit + 3] = shear
    stiffness = np.zeros((24, 24))
    mass_small = np.zeros((8, 8))
    point = 1.0 / np.sqrt(3.0)
    for gauss in range(8):
        coords = [point * (2 * (gauss >> axis_bit & 1) - 1) for axis_bit in range(3)]
        shape_values = np.zeros(8)
        grads = np.zeros((3, 8))
        for corner in range(8):
            signs = [2 * (corner >> axis_bit & 1) - 1 for axis_bit in range(3)]
            factors = [1.0 + signs[axis_bit] * coords[axis_bit] for axis_bit in range(3)]
            shape_values[corner] = 0.125 * factors[0] * factors[1] * factors[2]
            grads[0, corner] = 0.25 * signs[0] * factors[1] * factors[2]
            grads[1, corner] = 0.25 * signs[1] * factors[0] * factors[2]
            grads[2, corner] = 0.25 * signs[2] * factors[0] * factors[1]
        strain = np.zeros((6, 24))
        for corner in range(8):
            column = 3 * corner
            strain[0, column] = grads[0, corner]
            strain[1, column + 1] = grads[1, corner]
            strain[2, column + 2] = grads[2, corner]
            strain[3, column] = grads[1, corner]
            strain[3, column + 1] = grads[0, corner]
            strain[4, column + 1] = grads[2, corner]
            strain[4, column + 2] = grads[1, corner]
            strain[5, column] = grads[2, corner]
            strain[5, column + 2] = grads[0, corner]
        stiffness = stiffness + strain.T @ elastic @ strain * 0.125
        mass_small = mass_small + np.outer(shape_values, shape_values) * 0.125
    mass = np.kron(mass_small, np.eye(3))
    return np.concatenate([stiffness, mass], 0).astype(np.float32)


def rounded_tables():
    table = element_tables().astype(ml_dtypes.bfloat16).astype(np.float32)
    return table[:24], table[24:]


def sector_tables():
    stiff_matrix, mass_matrix = rounded_tables()
    walsh = np.array([[(-1) ** bin(s & c).count("1") for c in range(8)] for s in range(8)], np.float64)
    full = np.kron(walsh, np.eye(3))
    back = full.T / 8.0
    assert np.array_equal(full @ back, np.eye(24))
    stiff = back.T @ stiff_matrix.astype(np.float64) @ back
    mass = back.T @ mass_matrix.astype(np.float64) @ back
    blocks = np.zeros((8, 3, 3))
    kept = np.zeros_like(stiff, bool)
    for e in range(8):
        for k in range(3):
            for q in range(3):
                i = 3 * (e ^ (1 << k)) + k
                j = 3 * (e ^ (1 << q)) + q
                blocks[e, k, q] = stiff[i, j]
                kept[i, j] = True
    assert not np.any(stiff[~kept])
    diagonal = np.diag(mass).reshape(8, 3)
    assert not np.any(mass - np.diag(np.diag(mass)))
    assert np.all(diagonal == diagonal[:, :1])
    return blocks, diagonal[:, 0]


def walsh(values):
    values = list(values)
    for bit in (1, 2, 4):
        for c in range(8):
            if c & bit == 0:
                a, b = values[c], values[c | bit]
                values[c], values[c | bit] = a + b, a - b
    return values


def element_forms(u, blocks, weights):
    spectra = [walsh([u[3 * c + k] for c in range(8)]) for k in range(3)]
    stiff = None
    for e in range(8):
        z = [spectra[k][e ^ (1 << k)] for k in range(3)]
        for k in range(3):
            term = None
            for q in range(k, 3):
                coefficient = blocks[e, k, q] * (1.0 if q == k else 2.0)
                if coefficient == 0.0:
                    continue
                piece = float(coefficient) * z[q]
                term = piece if term is None else term + piece
            if term is None:
                continue
            piece = z[k] * term
            stiff = piece if stiff is None else stiff + piece
    mass = None
    for s in range(8):
        power = spectra[0][s] * spectra[0][s] + spectra[1][s] * spectra[1][s] + spectra[2][s] * spectra[2][s]
        piece = float(weights[s]) * power
        mass = piece if mass is None else mass + piece
    return stiff, mass


def filter_offsets():
    listed = []
    for z_step in range(-2, 3):
        for y_step in range(-2, 3):
            for x_step in range(-2, 3):
                weight = 2.5 - float(np.sqrt(z_step * z_step + y_step * y_step + x_step * x_step))
                if weight > 0.0:
                    listed.append((z_step, y_step, x_step, weight))
    return listed


def totals_table(depth, height, width, blocks):
    listed = filter_offsets()
    out = []
    for first_layer in (0, depth, (blocks - 1) * depth):
        total = np.zeros((depth, height, width), np.float64)
        for z in range(depth):
            for z_step, y_step, x_step, weight in listed:
                layer = first_layer + z + z_step
                if layer < 0 or layer >= blocks * depth:
                    continue
                ys = np.arange(height) + y_step
                xs = np.arange(width) + x_step
                inside = ((ys >= 0) & (ys < height))[:, None] & ((xs >= 0) & (xs < width))[None, :]
                total[z] += weight * inside
        out.append(total)
    return np.stack(out).astype(np.float32)


def form_kernel(modes_ref, upper_ref, dens_ref, tot_ref, eig_ref, case_ref, out_ref, sh_ref):
    count = modes_ref.shape[0]
    depth = modes_ref.shape[2]
    height = modes_ref.shape[3]
    width = modes_ref.shape[4]
    blocks, weights = sector_tables()
    lane = lax.broadcasted_iota(jnp.int32, (height, width), 1)
    row = lax.broadcasted_iota(jnp.int32, (height, width), 0)
    x_edge = lane == width - 1
    y_edge = row == height - 1

    def plane(m, k, p):
        if p < depth:
            return modes_ref[m, k, p].astype(jnp.float32)
        return upper_ref[m, k, 0].astype(jnp.float32)

    def prepare(m, carry):
        for k in range(3):
            for p in range(depth + 1):
                base = plane(m, k, p)
                along_x = jnp.where(x_edge, 0.0, pltpu.roll(base, width - 1, 1))
                along_y = jnp.where(y_edge, 0.0, pltpu.roll(base, height - 1, 0))
                along_xy = jnp.where(y_edge, 0.0, pltpu.roll(along_x, height - 1, 0))
                sh_ref[m, k, p, 0] = base
                sh_ref[m, k, p, 1] = along_x
                sh_ref[m, k, p, 2] = along_y
                sh_ref[m, k, p, 3] = along_xy
        return carry

    lax.fori_loop(0, count, prepare, 0)

    chunks = height // 8

    def accumulate(m, carry):
        value = eig_ref[m]
        new = []
        for layer in range(depth):
            for b in range(chunks):
                rows = slice(8 * b, 8 * b + 8)
                u = []
                for corner in range(8):
                    x_off = corner & 1
                    y_off = corner >> 1 & 1
                    z_off = corner >> 2
                    for k in range(3):
                        u.append(sh_ref[m, k, layer + z_off, x_off + 2 * y_off, rows, :])
                stiff, mass = element_forms(u, blocks, weights)
                at = 2 * (layer * chunks + b)
                new.append(carry[at] + stiff)
                new.append(carry[at + 1] + value * mass)
        return tuple(new)

    zero = jnp.zeros((8, width), jnp.float32)
    sums = lax.fori_loop(0, count, accumulate, tuple(zero for _ in range(2 * depth * chunks)))
    case = case_ref[0]
    for layer in range(depth):
        for b in range(chunks):
            rows = slice(8 * b, 8 * b + 8)
            at = 2 * (layer * chunks + b)
            density = dens_ref[layer, rows, :]
            slope = 3.0 * (1.0 - 0.001) * density * density
            sensitivity = slope * sums[at] - sums[at + 1]
            scaled = (sensitivity / tot_ref[case, layer, rows, :]).astype(out_ref.dtype)
            for copy in range(out_ref.shape[0]):
                out_ref[copy, layer, rows, :] = scaled


def element_pass(operands, copies, depth, height, width, count):
    vmem = pl.BlockSpec(memory_space=pltpu.VMEM)
    smem = pl.BlockSpec(memory_space=pltpu.SMEM)
    specs = [vmem] * (len(operands) - 2) + [smem, smem]
    return pl.pallas_call(
        form_kernel,
        out_shape=jax.ShapeDtypeStruct((copies, depth, height, width), jnp.bfloat16),
        in_specs=specs,
        out_specs=vmem,
        scratch_shapes=[pltpu.VMEM((count, 3, depth + 1, 4, height, width), jnp.float32)],
    )(*operands)


def stencil_bands(width):
    offsets = []
    bands = []
    for z_step in range(-2, 3):
        for y_step in range(-2, 3):
            band = np.zeros((width, width), np.float32)
            used = False
            for x_step in range(-2, 3):
                weight = 2.5 - float(np.sqrt(z_step * z_step + y_step * y_step + x_step * x_step))
                if weight > 0.0:
                    band = band + weight * np.eye(width, k=-x_step, dtype=np.float32)
                    used = True
            if used:
                offsets.append((z_step, y_step))
                bands.append(band)
    return (offsets, np.stack(bands))


def apply_stencil(padded, width):
    depth = padded.shape[0] - 4
    height = padded.shape[1] - 4
    offsets, bands = stencil_bands(width)
    stacked = jnp.stack(
        [
            padded[2 + z_step : 2 + z_step + depth, 2 + y_step : 2 + y_step + height, :]
            for z_step, y_step in offsets
        ]
    )
    return jnp.einsum(
        "kzyx,kxw->zyw",
        stacked,
        jnp.asarray(bands),
        precision=lax.Precision.HIGHEST,
        preferred_element_type=jnp.float32,
    )


def local(modes, eigenvalues, density):
    count = modes.shape[0]
    depth = density.shape[0]
    height = density.shape[1]
    width = density.shape[2]
    blocks = lax.axis_size("grid")
    g = lax.axis_index("grid")
    case = ((g > 0).astype(jnp.int32) + (g == blocks - 1).astype(jnp.int32)).reshape(1)
    totals = jnp.asarray(totals_table(depth, height, width, blocks))
    upper = shifted(modes[:, :, :1], "grid", -1)
    modes_count = lax.axis_size("mode")
    operands = (modes, upper, density, totals, eigenvalues, case)
    spread = element_pass(operands, modes_count, depth, height, width, count)
    got = lax.all_to_all(spread, "mode", 0, 0, tiled=False).astype(jnp.float32)
    block = (got[0] + got[1]) + (got[2] + got[3])
    halo = block.astype(jnp.bfloat16)
    low = shifted(halo, "grid", 1).astype(jnp.float32)
    high = shifted(halo, "grid", -1).astype(jnp.float32)
    widened = jnp.concatenate([low, block, high], 0)
    widened = jnp.pad(widened, ((0, 0), (2, 2), (0, 0)))
    return apply_stencil(widened, width)


def solution(mesh):
    in_specs = (P("mode", None, "grid", None, None), P("mode"), P("grid", None, None))
    out_specs = P("grid", None, None)
    return jax.shard_map(local, mesh=mesh, in_specs=in_specs, out_specs=out_specs, check_vma=False)
```

```python
import functools

import jax
import jax.numpy as jnp
import ml_dtypes
import numpy as np
from jax import lax
from jax.experimental import pallas as pl
from jax.experimental.pallas import tpu as pltpu
from jax.sharding import PartitionSpec as P


def shifted(value, axis, steps):
    count = lax.axis_size(axis)
    first, last = (max(0, -steps), min(count, count - steps))
    return lax.ppermute(value, axis, [(source, source + steps) for source in range(first, last)])


def element_tables():
    poisson = 0.3
    lame_first = poisson / ((1.0 + poisson) * (1.0 - 2.0 * poisson))
    shear = 0.5 / (1.0 + poisson)
    elastic = np.zeros((6, 6))
    elastic[:3, :3] = lame_first
    for axis_bit in range(3):
        elastic[axis_bit, axis_bit] += 2.0 * shear
        elastic[axis_bit + 3, axis_bit + 3] = shear
    stiffness = np.zeros((24, 24))
    mass_small = np.zeros((8, 8))
    point = 1.0 / np.sqrt(3.0)
    for gauss in range(8):
        coords = [point * (2 * (gauss >> axis_bit & 1) - 1) for axis_bit in range(3)]
        shape_values = np.zeros(8)
        grads = np.zeros((3, 8))
        for corner in range(8):
            signs = [2 * (corner >> axis_bit & 1) - 1 for axis_bit in range(3)]
            factors = [1.0 + signs[axis_bit] * coords[axis_bit] for axis_bit in range(3)]
            shape_values[corner] = 0.125 * factors[0] * factors[1] * factors[2]
            grads[0, corner] = 0.25 * signs[0] * factors[1] * factors[2]
            grads[1, corner] = 0.25 * signs[1] * factors[0] * factors[2]
            grads[2, corner] = 0.25 * signs[2] * factors[0] * factors[1]
        strain = np.zeros((6, 24))
        for corner in range(8):
            column = 3 * corner
            strain[0, column] = grads[0, corner]
            strain[1, column + 1] = grads[1, corner]
            strain[2, column + 2] = grads[2, corner]
            strain[3, column] = grads[1, corner]
            strain[3, column + 1] = grads[0, corner]
            strain[4, column + 1] = grads[2, corner]
            strain[4, column + 2] = grads[1, corner]
            strain[5, column] = grads[2, corner]
            strain[5, column + 2] = grads[0, corner]
        stiffness = stiffness + strain.T @ elastic @ strain * 0.125
        mass_small = mass_small + np.outer(shape_values, shape_values) * 0.125
    mass = np.kron(mass_small, np.eye(3))
    return np.concatenate([stiffness, mass], 0).astype(np.float32)


def rounded_tables():
    table = element_tables().astype(ml_dtypes.bfloat16).astype(np.float32)
    return table[:24], table[24:]


def sector_tables():
    stiff_matrix, mass_matrix = rounded_tables()
    walsh = np.array([[(-1) ** bin(s & c).count("1") for c in range(8)] for s in range(8)], np.float64)
    full = np.kron(walsh, np.eye(3))
    back = full.T / 8.0
    assert np.array_equal(full @ back, np.eye(24))
    stiff = back.T @ stiff_matrix.astype(np.float64) @ back
    mass = back.T @ mass_matrix.astype(np.float64) @ back
    blocks = np.zeros((8, 3, 3))
    kept = np.zeros_like(stiff, bool)
    for e in range(8):
        for k in range(3):
            for q in range(3):
                i = 3 * (e ^ (1 << k)) + k
                j = 3 * (e ^ (1 << q)) + q
                blocks[e, k, q] = stiff[i, j]
                kept[i, j] = True
    assert not np.any(stiff[~kept])
    diagonal = np.diag(mass).reshape(8, 3)
    assert not np.any(mass - np.diag(np.diag(mass)))
    assert np.all(diagonal == diagonal[:, :1])
    return blocks, diagonal[:, 0]


def walsh(values):
    values = list(values)
    for bit in (1, 2, 4):
        for c in range(8):
            if c & bit == 0:
                a, b = values[c], values[c | bit]
                values[c], values[c | bit] = a + b, a - b
    return values


def element_forms(u, blocks, weights):
    spectra = [walsh([u[3 * c + k] for c in range(8)]) for k in range(3)]
    stiff = None
    for e in range(8):
        z = [spectra[k][e ^ (1 << k)] for k in range(3)]
        for k in range(3):
            term = None
            for q in range(k, 3):
                coefficient = blocks[e, k, q] * (1.0 if q == k else 2.0)
                if coefficient == 0.0:
                    continue
                piece = float(coefficient) * z[q]
                term = piece if term is None else term + piece
            if term is None:
                continue
            piece = z[k] * term
            stiff = piece if stiff is None else stiff + piece
    mass = None
    for s in range(8):
        power = spectra[0][s] * spectra[0][s] + spectra[1][s] * spectra[1][s] + spectra[2][s] * spectra[2][s]
        piece = float(weights[s]) * power
        mass = piece if mass is None else mass + piece
    return stiff, mass


def filter_offsets():
    listed = []
    for z_step in range(-2, 3):
        for y_step in range(-2, 3):
            for x_step in range(-2, 3):
                weight = 2.5 - float(np.sqrt(z_step * z_step + y_step * y_step + x_step * x_step))
                if weight > 0.0:
                    listed.append((z_step, y_step, x_step, weight))
    return listed


def totals_table(depth, height, width, blocks):
    listed = filter_offsets()
    out = []
    for first_layer in (0, depth, (blocks - 1) * depth):
        total = np.zeros((depth, height, width), np.float64)
        for z in range(depth):
            for z_step, y_step, x_step, weight in listed:
                layer = first_layer + z + z_step
                if layer < 0 or layer >= blocks * depth:
                    continue
                ys = np.arange(height) + y_step
                xs = np.arange(width) + x_step
                inside = ((ys >= 0) & (ys < height))[:, None] & ((xs >= 0) & (xs < width))[None, :]
                total[z] += weight * inside
        out.append(total)
    return np.stack(out).astype(np.float32)


def form_kernel(layer, *refs):
    if layer == 0:
        modes_ref, dens_ref, tot_ref, eig_ref, case_ref, out_ref, sh_ref = refs
    else:
        modes_ref, upper_ref, prev_ref, dens_ref, tot_ref, eig_ref, case_ref, out_ref, sh_ref, up_ref = refs
        pltpu.sync_copy(upper_ref, up_ref)
    count = modes_ref.shape[0]
    depth = modes_ref.shape[2]
    height = modes_ref.shape[3]
    width = modes_ref.shape[4]
    blocks, weights = sector_tables()
    lane = lax.broadcasted_iota(jnp.int32, (height, width), 1)
    row = lax.broadcasted_iota(jnp.int32, (height, width), 0)
    x_edge = lane == width - 1
    y_edge = row == height - 1

    def plane(m, k, p):
        if layer + p < depth:
            return modes_ref[m, k, layer + p].astype(jnp.float32)
        return up_ref[m, k, 0].astype(jnp.float32)

    def prepare(m, carry):
        for k in range(3):
            for p in range(2):
                base = plane(m, k, p)
                along_x = jnp.where(x_edge, 0.0, pltpu.roll(base, width - 1, 1))
                along_y = jnp.where(y_edge, 0.0, pltpu.roll(base, height - 1, 0))
                along_xy = jnp.where(y_edge, 0.0, pltpu.roll(along_x, height - 1, 0))
                sh_ref[m, k, p, 0] = base
                sh_ref[m, k, p, 1] = along_x
                sh_ref[m, k, p, 2] = along_y
                sh_ref[m, k, p, 3] = along_xy
        return carry

    lax.fori_loop(0, count, prepare, 0)

    chunks = height // 8

    def accumulate(m, carry):
        value = eig_ref[m]
        new = []
        for b in range(chunks):
            rows = slice(8 * b, 8 * b + 8)
            u = []
            for corner in range(8):
                x_off = corner & 1
                y_off = corner >> 1 & 1
                z_off = corner >> 2
                for k in range(3):
                    u.append(sh_ref[m, k, z_off, x_off + 2 * y_off, rows, :])
            stiff, mass = element_forms(u, blocks, weights)
            new.append(carry[2 * b] + stiff)
            new.append(carry[2 * b + 1] + value * mass)
        return tuple(new)

    zero = jnp.zeros((8, width), jnp.float32)
    sums = lax.fori_loop(0, count, accumulate, tuple(zero for _ in range(2 * chunks)))
    case = case_ref[0]
    if layer > 0:
        out_ref[:, :layer] = prev_ref[...]
    for b in range(chunks):
        rows = slice(8 * b, 8 * b + 8)
        density = dens_ref[layer, rows, :]
        slope = 3.0 * (1.0 - 0.001) * density * density
        sensitivity = slope * sums[2 * b] - sums[2 * b + 1]
        scaled = (sensitivity / tot_ref[case, layer, rows, :]).astype(out_ref.dtype)
        for copy in range(out_ref.shape[0]):
            out_ref[copy, layer, rows, :] = scaled


def element_pass(layer, operands, copies, height, width, count):
    vmem = pl.BlockSpec(memory_space=pltpu.VMEM)
    smem = pl.BlockSpec(memory_space=pltpu.SMEM)
    anywhere = pl.BlockSpec(memory_space=pl.ANY)
    scratch = [pltpu.VMEM((count, 3, 2, 4, height, width), jnp.float32)]
    if layer == 0:
        specs = [vmem] * 3 + [smem, smem]
    else:
        specs = [vmem, anywhere] + [vmem] * 3 + [smem, smem]
        scratch.append(pltpu.VMEM(operands[1].shape, operands[1].dtype))
    return pl.pallas_call(
        functools.partial(form_kernel, layer),
        out_shape=jax.ShapeDtypeStruct((copies, layer + 1, height, width), jnp.bfloat16),
        in_specs=specs,
        out_specs=vmem,
        scratch_shapes=scratch,
    )(*operands)


def stencil_bands(width):
    offsets = []
    bands = []
    for z_step in range(-2, 3):
        for y_step in range(-2, 3):
            band = np.zeros((width, width), np.float32)
            used = False
            for x_step in range(-2, 3):
                weight = 2.5 - float(np.sqrt(z_step * z_step + y_step * y_step + x_step * x_step))
                if weight > 0.0:
                    band = band + weight * np.eye(width, k=-x_step, dtype=np.float32)
                    used = True
            if used:
                offsets.append((z_step, y_step))
                bands.append(band)
    return (offsets, np.stack(bands))


def apply_stencil(padded, width):
    depth = padded.shape[0] - 4
    height = padded.shape[1] - 4
    offsets, bands = stencil_bands(width)
    stacked = jnp.stack(
        [
            padded[2 + z_step : 2 + z_step + depth, 2 + y_step : 2 + y_step + height, :]
            for z_step, y_step in offsets
        ]
    )
    return jnp.einsum(
        "kzyx,kxw->zyw",
        stacked,
        jnp.asarray(bands),
        precision=lax.Precision.HIGHEST,
        preferred_element_type=jnp.float32,
    )


def local(modes, eigenvalues, density):
    count = modes.shape[0]
    depth = density.shape[0]
    height = density.shape[1]
    width = density.shape[2]
    blocks = lax.axis_size("grid")
    g = lax.axis_index("grid")
    case = ((g > 0).astype(jnp.int32) + (g == blocks - 1).astype(jnp.int32)).reshape(1)
    totals = jnp.asarray(totals_table(depth, height, width, blocks))
    upper = shifted(modes[:, :, :1], "grid", -1)
    modes_count = lax.axis_size("mode")
    first = element_pass(0, (modes, density, totals, eigenvalues, case), modes_count, height, width, count)
    operands = (modes, upper, first, density, totals, eigenvalues, case)
    spread = element_pass(1, operands, modes_count, height, width, count)
    got = lax.all_to_all(spread, "mode", 0, 0, tiled=False).astype(jnp.float32)
    block = (got[0] + got[1]) + (got[2] + got[3])
    halo = block.astype(jnp.bfloat16)
    low = shifted(halo, "grid", 1).astype(jnp.float32)
    high = shifted(halo, "grid", -1).astype(jnp.float32)
    widened = jnp.concatenate([low, block, high], 0)
    widened = jnp.pad(widened, ((0, 0), (2, 2), (0, 0)))
    return apply_stencil(widened, width)


def solution(mesh):
    in_specs = (P("mode", None, "grid", None, None), P("mode"), P("grid", None, None))
    out_specs = P("grid", None, None)
    return jax.shard_map(local, mesh=mesh, in_specs=in_specs, out_specs=out_specs, check_vma=False)
```

```python
import functools

import jax
import jax.numpy as jnp
import ml_dtypes
import numpy as np
from jax import lax
from jax.experimental import pallas as pl
from jax.experimental.pallas import tpu as pltpu
from jax.sharding import PartitionSpec as P


def shifted(value, axis, steps):
    count = lax.axis_size(axis)
    first, last = (max(0, -steps), min(count, count - steps))
    return lax.ppermute(value, axis, [(source, source + steps) for source in range(first, last)])


def element_tables():
    poisson = 0.3
    lame_first = poisson / ((1.0 + poisson) * (1.0 - 2.0 * poisson))
    shear = 0.5 / (1.0 + poisson)
    elastic = np.zeros((6, 6))
    elastic[:3, :3] = lame_first
    for axis_bit in range(3):
        elastic[axis_bit, axis_bit] += 2.0 * shear
        elastic[axis_bit + 3, axis_bit + 3] = shear
    stiffness = np.zeros((24, 24))
    mass_small = np.zeros((8, 8))
    point = 1.0 / np.sqrt(3.0)
    for gauss in range(8):
        coords = [point * (2 * (gauss >> axis_bit & 1) - 1) for axis_bit in range(3)]
        shape_values = np.zeros(8)
        grads = np.zeros((3, 8))
        for corner in range(8):
            signs = [2 * (corner >> axis_bit & 1) - 1 for axis_bit in range(3)]
            factors = [1.0 + signs[axis_bit] * coords[axis_bit] for axis_bit in range(3)]
            shape_values[corner] = 0.125 * factors[0] * factors[1] * factors[2]
            grads[0, corner] = 0.25 * signs[0] * factors[1] * factors[2]
            grads[1, corner] = 0.25 * signs[1] * factors[0] * factors[2]
            grads[2, corner] = 0.25 * signs[2] * factors[0] * factors[1]
        strain = np.zeros((6, 24))
        for corner in range(8):
            column = 3 * corner
            strain[0, column] = grads[0, corner]
            strain[1, column + 1] = grads[1, corner]
            strain[2, column + 2] = grads[2, corner]
            strain[3, column] = grads[1, corner]
            strain[3, column + 1] = grads[0, corner]
            strain[4, column + 1] = grads[2, corner]
            strain[4, column + 2] = grads[1, corner]
            strain[5, column] = grads[2, corner]
            strain[5, column + 2] = grads[0, corner]
        stiffness = stiffness + strain.T @ elastic @ strain * 0.125
        mass_small = mass_small + np.outer(shape_values, shape_values) * 0.125
    mass = np.kron(mass_small, np.eye(3))
    return np.concatenate([stiffness, mass], 0).astype(np.float32)


def rounded_tables():
    table = element_tables().astype(ml_dtypes.bfloat16).astype(np.float32)
    return table[:24], table[24:]


def sector_tables():
    stiff_matrix, mass_matrix = rounded_tables()
    walsh = np.array([[(-1) ** bin(s & c).count("1") for c in range(8)] for s in range(8)], np.float64)
    full = np.kron(walsh, np.eye(3))
    back = full.T / 8.0
    assert np.array_equal(full @ back, np.eye(24))
    stiff = back.T @ stiff_matrix.astype(np.float64) @ back
    mass = back.T @ mass_matrix.astype(np.float64) @ back
    blocks = np.zeros((8, 3, 3))
    kept = np.zeros_like(stiff, bool)
    for e in range(8):
        for k in range(3):
            for q in range(3):
                i = 3 * (e ^ (1 << k)) + k
                j = 3 * (e ^ (1 << q)) + q
                blocks[e, k, q] = stiff[i, j]
                kept[i, j] = True
    assert not np.any(stiff[~kept])
    diagonal = np.diag(mass).reshape(8, 3)
    assert not np.any(mass - np.diag(np.diag(mass)))
    assert np.all(diagonal == diagonal[:, :1])
    return blocks, diagonal[:, 0]


def walsh(values):
    values = list(values)
    for bit in (1, 2, 4):
        for c in range(8):
            if c & bit == 0:
                a, b = values[c], values[c | bit]
                values[c], values[c | bit] = a + b, a - b
    return values


def element_forms(u, blocks, weights):
    spectra = [walsh([u[3 * c + k] for c in range(8)]) for k in range(3)]
    stiff = None
    for e in range(8):
        z = [spectra[k][e ^ (1 << k)] for k in range(3)]
        for k in range(3):
            term = None
            for q in range(k, 3):
                coefficient = blocks[e, k, q] * (1.0 if q == k else 2.0)
                if coefficient == 0.0:
                    continue
                piece = float(coefficient) * z[q]
                term = piece if term is None else term + piece
            if term is None:
                continue
            piece = z[k] * term
            stiff = piece if stiff is None else stiff + piece
    mass = None
    for s in range(8):
        power = spectra[0][s] * spectra[0][s] + spectra[1][s] * spectra[1][s] + spectra[2][s] * spectra[2][s]
        piece = float(weights[s]) * power
        mass = piece if mass is None else mass + piece
    return stiff, mass


def filter_offsets():
    listed = []
    for z_step in range(-2, 3):
        for y_step in range(-2, 3):
            for x_step in range(-2, 3):
                weight = 2.5 - float(np.sqrt(z_step * z_step + y_step * y_step + x_step * x_step))
                if weight > 0.0:
                    listed.append((z_step, y_step, x_step, weight))
    return listed


def totals_table(depth, height, width, blocks):
    listed = filter_offsets()
    out = []
    for first_layer in (0, depth, (blocks - 1) * depth):
        total = np.zeros((depth, height, width), np.float64)
        for z in range(depth):
            for z_step, y_step, x_step, weight in listed:
                layer = first_layer + z + z_step
                if layer < 0 or layer >= blocks * depth:
                    continue
                ys = np.arange(height) + y_step
                xs = np.arange(width) + x_step
                inside = ((ys >= 0) & (ys < height))[:, None] & ((xs >= 0) & (xs < width))[None, :]
                total[z] += weight * inside
        out.append(total)
    return np.stack(out).astype(np.float32)


def form_kernel(layer, *refs):
    if layer == 0:
        modes_ref, dens_ref, tot_ref, eig_ref, case_ref, out_ref, sh_ref = refs
    else:
        modes_ref, upper_ref, prev_ref, dens_ref, tot_ref, eig_ref, case_ref, out_ref, sh_ref, up_ref = refs
        pltpu.sync_copy(upper_ref, up_ref)
    count = modes_ref.shape[0]
    depth = modes_ref.shape[2]
    height = modes_ref.shape[3]
    width = modes_ref.shape[4]
    blocks, weights = sector_tables()
    lane = lax.broadcasted_iota(jnp.int32, (height, width), 1)
    row = lax.broadcasted_iota(jnp.int32, (height, width), 0)
    x_edge = lane == width - 1
    y_edge = row == height - 1

    def plane(m, k, p):
        if layer + p < depth:
            return modes_ref[m, k, layer + p].astype(jnp.float32)
        return up_ref[m, k, 0].astype(jnp.float32)

    def prepare(m, carry):
        for k in range(3):
            for p in range(2):
                base = plane(m, k, p)
                along_x = jnp.where(x_edge, 0.0, pltpu.roll(base, width - 1, 1))
                along_y = jnp.where(y_edge, 0.0, pltpu.roll(base, height - 1, 0))
                along_xy = jnp.where(y_edge, 0.0, pltpu.roll(along_x, height - 1, 0))
                sh_ref[m, k, p, 0] = base
                sh_ref[m, k, p, 1] = along_x
                sh_ref[m, k, p, 2] = along_y
                sh_ref[m, k, p, 3] = along_xy
        return carry

    lax.fori_loop(0, count, prepare, 0)

    chunks = height // 8

    def accumulate(m, carry):
        value = eig_ref[m]
        new = []
        for b in range(chunks):
            rows = slice(8 * b, 8 * b + 8)
            u = []
            for corner in range(8):
                x_off = corner & 1
                y_off = corner >> 1 & 1
                z_off = corner >> 2
                for k in range(3):
                    u.append(sh_ref[m, k, z_off, x_off + 2 * y_off, rows, :])
            stiff, mass = element_forms(u, blocks, weights)
            new.append(carry[2 * b] + stiff)
            new.append(carry[2 * b + 1] + value * mass)
        return tuple(new)

    zero = jnp.zeros((8, width), jnp.float32)
    sums = lax.fori_loop(0, count, accumulate, tuple(zero for _ in range(2 * chunks)))
    case = case_ref[0]
    if layer > 0:
        out_ref[:, :layer] = prev_ref[...]
    for b in range(chunks):
        rows = slice(8 * b, 8 * b + 8)
        density = dens_ref[layer, rows, :]
        slope = 3.0 * (1.0 - 0.001) * density * density
        sensitivity = slope * sums[2 * b] - sums[2 * b + 1]
        scaled = (sensitivity / tot_ref[case, layer, rows, :]).astype(out_ref.dtype)
        for copy in range(out_ref.shape[0]):
            out_ref[copy, layer, rows, :] = scaled


def element_pass(layer, operands, copies, height, width, count):
    vmem = pl.BlockSpec(memory_space=pltpu.VMEM)
    smem = pl.BlockSpec(memory_space=pltpu.SMEM)
    anywhere = pl.BlockSpec(memory_space=pl.ANY)
    scratch = [pltpu.VMEM((count, 3, 2, 4, height, width), jnp.float32)]
    if layer == 0:
        specs = [vmem] * 3 + [smem, smem]
    else:
        specs = [vmem, anywhere] + [vmem] * 3 + [smem, smem]
        scratch.append(pltpu.VMEM(operands[1].shape, operands[1].dtype))
    return pl.pallas_call(
        functools.partial(form_kernel, layer),
        out_shape=jax.ShapeDtypeStruct((copies, layer + 1, height, width), jnp.bfloat16),
        in_specs=specs,
        out_specs=vmem,
        scratch_shapes=scratch,
    )(*operands)


def stencil_bands(width):
    offsets = []
    bands = []
    for z_step in range(-2, 3):
        for y_step in range(-2, 3):
            band = np.zeros((width, width), np.float32)
            used = False
            for x_step in range(-2, 3):
                weight = 2.5 - float(np.sqrt(z_step * z_step + y_step * y_step + x_step * x_step))
                if weight > 0.0:
                    band = band + weight * np.eye(width, k=-x_step, dtype=np.float32)
                    used = True
            if used:
                offsets.append((z_step, y_step))
                bands.append(band)
    return (offsets, np.stack(bands))


def apply_stencil(padded, width):
    depth = padded.shape[0] - 4
    height = padded.shape[1] - 4
    offsets, bands = stencil_bands(width)
    high = bands.astype(ml_dtypes.bfloat16)
    low = (bands - high.astype(np.float32)).astype(ml_dtypes.bfloat16)
    stacked = jnp.stack(
        [
            padded[2 + z_step : 2 + z_step + depth, 2 + y_step : 2 + y_step + height, :]
            for z_step, y_step in offsets
        ]
    )
    parts = [
        jnp.einsum("kzyx,kxw->zyw", stacked, jnp.asarray(part), preferred_element_type=jnp.float32)
        for part in (high, low)
    ]
    return parts[0] + parts[1]


def local(modes, eigenvalues, density):
    count = modes.shape[0]
    depth = density.shape[0]
    height = density.shape[1]
    width = density.shape[2]
    blocks = lax.axis_size("grid")
    g = lax.axis_index("grid")
    case = ((g > 0).astype(jnp.int32) + (g == blocks - 1).astype(jnp.int32)).reshape(1)
    totals = jnp.asarray(totals_table(depth, height, width, blocks))
    upper = shifted(modes[:, :, :1], "grid", -1)
    modes_count = lax.axis_size("mode")
    first = element_pass(0, (modes, density, totals, eigenvalues, case), modes_count, height, width, count)
    operands = (modes, upper, first, density, totals, eigenvalues, case)
    spread = element_pass(1, operands, modes_count, height, width, count)
    got = lax.all_to_all(spread, "mode", 0, 0, tiled=False).astype(jnp.float32)
    block = (got[0] + got[1]) + (got[2] + got[3])
    halo = block.astype(jnp.bfloat16)
    low = shifted(halo, "grid", 1)
    high = shifted(halo, "grid", -1)
    widened = jnp.concatenate([low, halo, high], 0)
    widened = jnp.pad(widened, ((0, 0), (2, 2), (0, 0)))
    return apply_stencil(widened, width)


def solution(mesh):
    in_specs = (P("mode", None, "grid", None, None), P("mode"), P("grid", None, None))
    out_specs = P("grid", None, None)
    return jax.shard_map(local, mesh=mesh, in_specs=in_specs, out_specs=out_specs, check_vma=False)
```

```python
import functools

import jax
import jax.numpy as jnp
import ml_dtypes
import numpy as np
from jax import lax
from jax.experimental import pallas as pl
from jax.experimental.pallas import tpu as pltpu
from jax.sharding import PartitionSpec as P


def shifted(value, axis, steps):
    count = lax.axis_size(axis)
    first, last = (max(0, -steps), min(count, count - steps))
    return lax.ppermute(value, axis, [(source, source + steps) for source in range(first, last)])


def element_tables():
    poisson = 0.3
    lame_first = poisson / ((1.0 + poisson) * (1.0 - 2.0 * poisson))
    shear = 0.5 / (1.0 + poisson)
    elastic = np.zeros((6, 6))
    elastic[:3, :3] = lame_first
    for axis_bit in range(3):
        elastic[axis_bit, axis_bit] += 2.0 * shear
        elastic[axis_bit + 3, axis_bit + 3] = shear
    stiffness = np.zeros((24, 24))
    mass_small = np.zeros((8, 8))
    point = 1.0 / np.sqrt(3.0)
    for gauss in range(8):
        coords = [point * (2 * (gauss >> axis_bit & 1) - 1) for axis_bit in range(3)]
        shape_values = np.zeros(8)
        grads = np.zeros((3, 8))
        for corner in range(8):
            signs = [2 * (corner >> axis_bit & 1) - 1 for axis_bit in range(3)]
            factors = [1.0 + signs[axis_bit] * coords[axis_bit] for axis_bit in range(3)]
            shape_values[corner] = 0.125 * factors[0] * factors[1] * factors[2]
            grads[0, corner] = 0.25 * signs[0] * factors[1] * factors[2]
            grads[1, corner] = 0.25 * signs[1] * factors[0] * factors[2]
            grads[2, corner] = 0.25 * signs[2] * factors[0] * factors[1]
        strain = np.zeros((6, 24))
        for corner in range(8):
            column = 3 * corner
            strain[0, column] = grads[0, corner]
            strain[1, column + 1] = grads[1, corner]
            strain[2, column + 2] = grads[2, corner]
            strain[3, column] = grads[1, corner]
            strain[3, column + 1] = grads[0, corner]
            strain[4, column + 1] = grads[2, corner]
            strain[4, column + 2] = grads[1, corner]
            strain[5, column] = grads[2, corner]
            strain[5, column + 2] = grads[0, corner]
        stiffness = stiffness + strain.T @ elastic @ strain * 0.125
        mass_small = mass_small + np.outer(shape_values, shape_values) * 0.125
    mass = np.kron(mass_small, np.eye(3))
    return np.concatenate([stiffness, mass], 0).astype(np.float32)


def rounded_tables():
    table = element_tables().astype(ml_dtypes.bfloat16).astype(np.float32)
    return table[:24], table[24:]


def sector_tables():
    stiff_matrix, mass_matrix = rounded_tables()
    walsh = np.array([[(-1) ** bin(s & c).count("1") for c in range(8)] for s in range(8)], np.float64)
    full = np.kron(walsh, np.eye(3))
    back = full.T / 8.0
    assert np.array_equal(full @ back, np.eye(24))
    stiff = back.T @ stiff_matrix.astype(np.float64) @ back
    mass = back.T @ mass_matrix.astype(np.float64) @ back
    blocks = np.zeros((8, 3, 3))
    kept = np.zeros_like(stiff, bool)
    for e in range(8):
        for k in range(3):
            for q in range(3):
                i = 3 * (e ^ (1 << k)) + k
                j = 3 * (e ^ (1 << q)) + q
                blocks[e, k, q] = stiff[i, j]
                kept[i, j] = True
    assert not np.any(stiff[~kept])
    diagonal = np.diag(mass).reshape(8, 3)
    assert not np.any(mass - np.diag(np.diag(mass)))
    assert np.all(diagonal == diagonal[:, :1])
    return blocks, diagonal[:, 0]


def walsh(values):
    values = list(values)
    for bit in (1, 2, 4):
        for c in range(8):
            if c & bit == 0:
                a, b = values[c], values[c | bit]
                values[c], values[c | bit] = a + b, a - b
    return values


def element_forms(u, blocks, weights):
    spectra = [walsh([u[3 * c + k] for c in range(8)]) for k in range(3)]
    stiff = None
    for e in range(8):
        z = [spectra[k][e ^ (1 << k)] for k in range(3)]
        for k in range(3):
            term = None
            for q in range(k, 3):
                coefficient = blocks[e, k, q] * (1.0 if q == k else 2.0)
                if coefficient == 0.0:
                    continue
                piece = float(coefficient) * z[q]
                term = piece if term is None else term + piece
            if term is None:
                continue
            piece = z[k] * term
            stiff = piece if stiff is None else stiff + piece
    mass = None
    for s in range(8):
        power = spectra[0][s] * spectra[0][s] + spectra[1][s] * spectra[1][s] + spectra[2][s] * spectra[2][s]
        piece = float(weights[s]) * power
        mass = piece if mass is None else mass + piece
    return stiff, mass


def filter_offsets():
    listed = []
    for z_step in range(-2, 3):
        for y_step in range(-2, 3):
            for x_step in range(-2, 3):
                weight = 2.5 - float(np.sqrt(z_step * z_step + y_step * y_step + x_step * x_step))
                if weight > 0.0:
                    listed.append((z_step, y_step, x_step, weight))
    return listed


def totals_table(depth, height, width, blocks):
    listed = filter_offsets()
    out = []
    for first_layer in (0, depth, (blocks - 1) * depth):
        total = np.zeros((depth, height, width), np.float64)
        for z in range(depth):
            for z_step, y_step, x_step, weight in listed:
                layer = first_layer + z + z_step
                if layer < 0 or layer >= blocks * depth:
                    continue
                ys = np.arange(height) + y_step
                xs = np.arange(width) + x_step
                inside = ((ys >= 0) & (ys < height))[:, None] & ((xs >= 0) & (xs < width))[None, :]
                total[z] += weight * inside
        out.append(total)
    return np.stack(out).astype(np.float32)


def form_kernel(layer, *refs):
    if layer == 0:
        modes_ref, dens_ref, tot_ref, eig_ref, case_ref, out_ref, sh_ref = refs
    else:
        modes_ref, upper_ref, prev_ref, dens_ref, tot_ref, eig_ref, case_ref, out_ref, sh_ref, up_ref = refs
        pltpu.sync_copy(upper_ref, up_ref)
    count = modes_ref.shape[0]
    depth = modes_ref.shape[2]
    height = modes_ref.shape[3]
    width = modes_ref.shape[4]
    blocks, weights = sector_tables()
    lane = lax.broadcasted_iota(jnp.int32, (height, width), 1)
    row = lax.broadcasted_iota(jnp.int32, (height, width), 0)
    x_edge = lane == width - 1
    y_edge = row == height - 1

    def plane(m, k, p):
        if layer + p < depth:
            return modes_ref[m, k, layer + p].astype(jnp.float32)
        return up_ref[m, k, 0].astype(jnp.float32)

    def prepare(m, carry):
        for k in range(3):
            for p in range(2):
                base = plane(m, k, p)
                along_x = jnp.where(x_edge, 0.0, pltpu.roll(base, width - 1, 1))
                along_y = jnp.where(y_edge, 0.0, pltpu.roll(base, height - 1, 0))
                along_xy = jnp.where(y_edge, 0.0, pltpu.roll(along_x, height - 1, 0))
                sh_ref[m, k, p, 0] = base
                sh_ref[m, k, p, 1] = along_x
                sh_ref[m, k, p, 2] = along_y
                sh_ref[m, k, p, 3] = along_xy
        return carry

    lax.fori_loop(0, count, prepare, 0)

    chunks = height // 8

    def accumulate(m, carry):
        value = eig_ref[m]
        new = []
        for b in range(chunks):
            rows = slice(8 * b, 8 * b + 8)
            u = []
            for corner in range(8):
                x_off = corner & 1
                y_off = corner >> 1 & 1
                z_off = corner >> 2
                for k in range(3):
                    u.append(sh_ref[m, k, z_off, x_off + 2 * y_off, rows, :])
            stiff, mass = element_forms(u, blocks, weights)
            new.append(carry[2 * b] + stiff)
            new.append(carry[2 * b + 1] + value * mass)
        return tuple(new)

    zero = jnp.zeros((8, width), jnp.float32)
    sums = lax.fori_loop(0, count, accumulate, tuple(zero for _ in range(2 * chunks)))
    case = case_ref[0]
    if layer > 0:
        out_ref[:, :layer] = prev_ref[...]
    for b in range(chunks):
        rows = slice(8 * b, 8 * b + 8)
        density = dens_ref[layer, rows, :]
        slope = 3.0 * (1.0 - 0.001) * density * density
        sensitivity = slope * sums[2 * b] - sums[2 * b + 1]
        scaled = (sensitivity / tot_ref[case, layer, rows, :]).astype(out_ref.dtype)
        for copy in range(out_ref.shape[0]):
            out_ref[copy, layer, rows, :] = scaled


def element_pass(layer, operands, copies, height, width, count):
    vmem = pl.BlockSpec(memory_space=pltpu.VMEM)
    smem = pl.BlockSpec(memory_space=pltpu.SMEM)
    anywhere = pl.BlockSpec(memory_space=pl.ANY)
    scratch = [pltpu.VMEM((count, 3, 2, 4, height, width), jnp.float32)]
    if layer == 0:
        specs = [vmem] * 3 + [smem, smem]
    else:
        specs = [vmem, anywhere] + [vmem] * 3 + [smem, smem]
        scratch.append(pltpu.VMEM(operands[1].shape, operands[1].dtype))
    return pl.pallas_call(
        functools.partial(form_kernel, layer),
        out_shape=jax.ShapeDtypeStruct((copies, layer + 1, height, width), jnp.bfloat16),
        in_specs=specs,
        out_specs=vmem,
        scratch_shapes=scratch,
    )(*operands)


def stencil_bands(width):
    offsets = []
    bands = []
    for z_step in range(-2, 3):
        for y_step in range(-2, 3):
            band = np.zeros((width, width), np.float32)
            used = False
            for x_step in range(-2, 3):
                weight = 2.5 - float(np.sqrt(z_step * z_step + y_step * y_step + x_step * x_step))
                if weight > 0.0:
                    band = band + weight * np.eye(width, k=-x_step, dtype=np.float32)
                    used = True
            if used:
                offsets.append((z_step, y_step))
                bands.append(band)
    return (offsets, np.stack(bands))


def apply_stencil(padded, width):
    depth = padded.shape[0] - 4
    height = padded.shape[1] - 4
    offsets, bands = stencil_bands(width)
    stacked = jnp.stack(
        [
            padded[2 + z_step : 2 + z_step + depth, 2 + y_step : 2 + y_step + height, :]
            for z_step, y_step in offsets
        ]
    )
    return jnp.einsum(
        "kzyx,kxw->zyw",
        stacked,
        jnp.asarray(bands),
        precision=lax.Precision.HIGHEST,
        preferred_element_type=jnp.float32,
    )


def local(modes, eigenvalues, density):
    count = modes.shape[0]
    depth = density.shape[0]
    height = density.shape[1]
    width = density.shape[2]
    blocks = lax.axis_size("grid")
    g = lax.axis_index("grid")
    case = ((g > 0).astype(jnp.int32) + (g == blocks - 1).astype(jnp.int32)).reshape(1)
    totals = jnp.asarray(totals_table(depth, height, width, blocks))
    upper = shifted(modes[:, :, :1], "grid", -1)
    modes_count = lax.axis_size("mode")
    first = element_pass(0, (modes, density, totals, eigenvalues, case), modes_count, height, width, count)
    operands = (modes, upper, first, density, totals, eigenvalues, case)
    spread = element_pass(1, operands, modes_count, height, width, count)
    got = lax.all_to_all(spread, "mode", 0, 0, tiled=False).astype(jnp.float32)
    block = (got[0] + got[1]) + (got[2] + got[3])
    halo = block.astype(jnp.bfloat16)
    own = jnp.pad(block, ((2, 2), (2, 2), (0, 0)))
    inner, halo = lax.optimization_barrier((apply_stencil(own, width), halo))
    low = shifted(halo, "grid", 1)
    high = shifted(halo, "grid", -1)
    return inner + halo_stencil(low, high, width)


def halo_stencil(low, high, width):
    depth = low.shape[0]
    height = low.shape[1]
    around = jnp.pad(jnp.concatenate([low, high], 0), ((0, 0), (2, 2), (0, 0)))
    pieces = []
    bands = []
    for z in range(depth):
        for source in range(2 * depth):
            layer = source - depth if source < depth else source
            z_step = layer - z
            for y_step in range(-2, 3):
                band = np.zeros((width, width), np.float32)
                used = False
                for x_step in range(-2, 3):
                    weight = 2.5 - float(np.sqrt(z_step * z_step + y_step * y_step + x_step * x_step))
                    if weight > 0.0:
                        band = band + weight * np.eye(width, k=-x_step, dtype=np.float32)
                        used = True
                if used:
                    pieces.append((z, source, y_step))
                    bands.append(band)
    rows = []
    for z in range(depth):
        chosen = [i for i, piece in enumerate(pieces) if piece[0] == z]
        stacked = jnp.stack([around[pieces[i][1], 2 + pieces[i][2] : 2 + pieces[i][2] + height] for i in chosen])
        rows.append(
            jnp.einsum(
                "kyx,kxw->yw",
                stacked,
                jnp.asarray(np.stack([bands[i] for i in chosen])),
                precision=lax.Precision.HIGH,
                preferred_element_type=jnp.float32,
            )
        )
    return jnp.stack(rows)


def solution(mesh):
    in_specs = (P("mode", None, "grid", None, None), P("mode"), P("grid", None, None))
    out_specs = P("grid", None, None)
    return jax.shard_map(local, mesh=mesh, in_specs=in_specs, out_specs=out_specs, check_vma=False)
```

```python
import functools

import jax
import jax.numpy as jnp
import ml_dtypes
import numpy as np
from jax import lax
from jax.experimental import pallas as pl
from jax.experimental.pallas import tpu as pltpu
from jax.sharding import PartitionSpec as P


def shifted(value, axis, steps):
    count = lax.axis_size(axis)
    first, last = (max(0, -steps), min(count, count - steps))
    return lax.ppermute(value, axis, [(source, source + steps) for source in range(first, last)])


def element_tables():
    poisson = 0.3
    lame_first = poisson / ((1.0 + poisson) * (1.0 - 2.0 * poisson))
    shear = 0.5 / (1.0 + poisson)
    elastic = np.zeros((6, 6))
    elastic[:3, :3] = lame_first
    for axis_bit in range(3):
        elastic[axis_bit, axis_bit] += 2.0 * shear
        elastic[axis_bit + 3, axis_bit + 3] = shear
    stiffness = np.zeros((24, 24))
    mass_small = np.zeros((8, 8))
    point = 1.0 / np.sqrt(3.0)
    for gauss in range(8):
        coords = [point * (2 * (gauss >> axis_bit & 1) - 1) for axis_bit in range(3)]
        shape_values = np.zeros(8)
        grads = np.zeros((3, 8))
        for corner in range(8):
            signs = [2 * (corner >> axis_bit & 1) - 1 for axis_bit in range(3)]
            factors = [1.0 + signs[axis_bit] * coords[axis_bit] for axis_bit in range(3)]
            shape_values[corner] = 0.125 * factors[0] * factors[1] * factors[2]
            grads[0, corner] = 0.25 * signs[0] * factors[1] * factors[2]
            grads[1, corner] = 0.25 * signs[1] * factors[0] * factors[2]
            grads[2, corner] = 0.25 * signs[2] * factors[0] * factors[1]
        strain = np.zeros((6, 24))
        for corner in range(8):
            column = 3 * corner
            strain[0, column] = grads[0, corner]
            strain[1, column + 1] = grads[1, corner]
            strain[2, column + 2] = grads[2, corner]
            strain[3, column] = grads[1, corner]
            strain[3, column + 1] = grads[0, corner]
            strain[4, column + 1] = grads[2, corner]
            strain[4, column + 2] = grads[1, corner]
            strain[5, column] = grads[2, corner]
            strain[5, column + 2] = grads[0, corner]
        stiffness = stiffness + strain.T @ elastic @ strain * 0.125
        mass_small = mass_small + np.outer(shape_values, shape_values) * 0.125
    mass = np.kron(mass_small, np.eye(3))
    return np.concatenate([stiffness, mass], 0).astype(np.float32)


def rounded_tables():
    table = element_tables().astype(ml_dtypes.bfloat16).astype(np.float32)
    return table[:24], table[24:]


def sector_tables():
    stiff_matrix, mass_matrix = rounded_tables()
    walsh = np.array([[(-1) ** bin(s & c).count("1") for c in range(8)] for s in range(8)], np.float64)
    full = np.kron(walsh, np.eye(3))
    back = full.T / 8.0
    assert np.array_equal(full @ back, np.eye(24))
    stiff = back.T @ stiff_matrix.astype(np.float64) @ back
    mass = back.T @ mass_matrix.astype(np.float64) @ back
    blocks = np.zeros((8, 3, 3))
    kept = np.zeros_like(stiff, bool)
    for e in range(8):
        for k in range(3):
            for q in range(3):
                i = 3 * (e ^ (1 << k)) + k
                j = 3 * (e ^ (1 << q)) + q
                blocks[e, k, q] = stiff[i, j]
                kept[i, j] = True
    assert not np.any(stiff[~kept])
    diagonal = np.diag(mass).reshape(8, 3)
    assert not np.any(mass - np.diag(np.diag(mass)))
    assert np.all(diagonal == diagonal[:, :1])
    return blocks, diagonal[:, 0]


def walsh(values):
    values = list(values)
    for bit in (1, 2, 4):
        for c in range(8):
            if c & bit == 0:
                a, b = values[c], values[c | bit]
                values[c], values[c | bit] = a + b, a - b
    return values


def element_forms(u, blocks, weights):
    spectra = [walsh([u[3 * c + k] for c in range(8)]) for k in range(3)]
    stiff = None
    for e in range(8):
        z = [spectra[k][e ^ (1 << k)] for k in range(3)]
        for k in range(3):
            term = None
            for q in range(k, 3):
                coefficient = blocks[e, k, q] * (1.0 if q == k else 2.0)
                if coefficient == 0.0:
                    continue
                piece = float(coefficient) * z[q]
                term = piece if term is None else term + piece
            if term is None:
                continue
            piece = z[k] * term
            stiff = piece if stiff is None else stiff + piece
    mass = None
    for s in range(8):
        power = spectra[0][s] * spectra[0][s] + spectra[1][s] * spectra[1][s] + spectra[2][s] * spectra[2][s]
        piece = float(weights[s]) * power
        mass = piece if mass is None else mass + piece
    return stiff, mass


def filter_offsets():
    listed = []
    for z_step in range(-2, 3):
        for y_step in range(-2, 3):
            for x_step in range(-2, 3):
                weight = 2.5 - float(np.sqrt(z_step * z_step + y_step * y_step + x_step * x_step))
                if weight > 0.0:
                    listed.append((z_step, y_step, x_step, weight))
    return listed


def totals_table(depth, height, width, blocks):
    listed = filter_offsets()
    out = []
    for first_layer in (0, depth, (blocks - 1) * depth):
        total = np.zeros((depth, height, width), np.float64)
        for z in range(depth):
            for z_step, y_step, x_step, weight in listed:
                layer = first_layer + z + z_step
                if layer < 0 or layer >= blocks * depth:
                    continue
                ys = np.arange(height) + y_step
                xs = np.arange(width) + x_step
                inside = ((ys >= 0) & (ys < height))[:, None] & ((xs >= 0) & (xs < width))[None, :]
                total[z] += weight * inside
        out.append(total)
    return np.stack(out).astype(np.float32)


def form_kernel(layer, *refs):
    if layer == 0:
        modes_ref, dens_ref, tot_ref, eig_ref, case_ref, out_ref, sh_ref = refs
    else:
        modes_ref, upper_ref, prev_ref, dens_ref, tot_ref, eig_ref, case_ref, out_ref, sh_ref, up_ref = refs
        pltpu.sync_copy(upper_ref, up_ref)
    count = modes_ref.shape[0]
    depth = modes_ref.shape[2]
    height = modes_ref.shape[3]
    width = modes_ref.shape[4]
    blocks, weights = sector_tables()
    lane = lax.broadcasted_iota(jnp.int32, (height, width), 1)
    row = lax.broadcasted_iota(jnp.int32, (height, width), 0)
    x_edge = lane == width - 1
    y_edge = row == height - 1

    def plane(m, k, p):
        if layer + p < depth:
            return modes_ref[m, k, layer + p].astype(jnp.float32)
        return up_ref[m, k, 0].astype(jnp.float32)

    def prepare(m, carry):
        for k in range(3):
            for p in range(2):
                base = plane(m, k, p)
                along_x = jnp.where(x_edge, 0.0, pltpu.roll(base, width - 1, 1))
                along_y = jnp.where(y_edge, 0.0, pltpu.roll(base, height - 1, 0))
                along_xy = jnp.where(y_edge, 0.0, pltpu.roll(along_x, height - 1, 0))
                sh_ref[m, k, p, 0] = base
                sh_ref[m, k, p, 1] = along_x
                sh_ref[m, k, p, 2] = along_y
                sh_ref[m, k, p, 3] = along_xy
        return carry

    lax.fori_loop(0, count, prepare, 0)

    chunks = height // 8

    def accumulate(m, carry):
        value = eig_ref[m]
        new = []
        for b in range(chunks):
            rows = slice(8 * b, 8 * b + 8)
            u = []
            for corner in range(8):
                x_off = corner & 1
                y_off = corner >> 1 & 1
                z_off = corner >> 2
                for k in range(3):
                    u.append(sh_ref[m, k, z_off, x_off + 2 * y_off, rows, :])
            stiff, mass = element_forms(u, blocks, weights)
            new.append(carry[2 * b] + stiff)
            new.append(carry[2 * b + 1] + value * mass)
        return tuple(new)

    zero = jnp.zeros((8, width), jnp.float32)
    sums = lax.fori_loop(0, count, accumulate, tuple(zero for _ in range(2 * chunks)))
    case = case_ref[0]
    if layer > 0:
        out_ref[:, :layer] = prev_ref[...]
    for b in range(chunks):
        rows = slice(8 * b, 8 * b + 8)
        density = dens_ref[layer, rows, :]
        slope = 3.0 * (1.0 - 0.001) * density * density
        sensitivity = slope * sums[2 * b] - sums[2 * b + 1]
        scaled = (sensitivity / tot_ref[case, layer, rows, :]).astype(out_ref.dtype)
        for copy in range(out_ref.shape[0]):
            out_ref[copy, layer, rows, :] = scaled


def element_pass(layer, operands, copies, height, width, count):
    vmem = pl.BlockSpec(memory_space=pltpu.VMEM)
    smem = pl.BlockSpec(memory_space=pltpu.SMEM)
    anywhere = pl.BlockSpec(memory_space=pl.ANY)
    scratch = [pltpu.VMEM((count, 3, 2, 4, height, width), jnp.float32)]
    if layer == 0:
        specs = [vmem] * 3 + [smem, smem]
    else:
        specs = [vmem, anywhere] + [vmem] * 3 + [smem, smem]
        scratch.append(pltpu.VMEM(operands[1].shape, operands[1].dtype))
    return pl.pallas_call(
        functools.partial(form_kernel, layer),
        out_shape=jax.ShapeDtypeStruct((copies, layer + 1, height, width), jnp.bfloat16),
        in_specs=specs,
        out_specs=vmem,
        scratch_shapes=scratch,
    )(*operands)


def stencil_bands(width):
    offsets = []
    bands = []
    for z_step in range(-2, 3):
        for y_step in range(-2, 3):
            band = np.zeros((width, width), np.float32)
            used = False
            for x_step in range(-2, 3):
                weight = 2.5 - float(np.sqrt(z_step * z_step + y_step * y_step + x_step * x_step))
                if weight > 0.0:
                    band = band + weight * np.eye(width, k=-x_step, dtype=np.float32)
                    used = True
            if used:
                offsets.append((z_step, y_step))
                bands.append(band)
    return (offsets, np.stack(bands))


def apply_stencil(padded, width):
    depth = padded.shape[0] - 4
    height = padded.shape[1] - 4
    offsets, bands = stencil_bands(width)
    stacked = jnp.stack(
        [
            padded[2 + z_step : 2 + z_step + depth, 2 + y_step : 2 + y_step + height, :]
            for z_step, y_step in offsets
        ]
    )
    return jnp.einsum(
        "kzyx,kxw->zyw",
        stacked,
        jnp.asarray(bands),
        precision=lax.Precision.HIGHEST,
        preferred_element_type=jnp.float32,
    )


def local(modes, eigenvalues, density):
    count = modes.shape[0]
    depth = density.shape[0]
    height = density.shape[1]
    width = density.shape[2]
    grid = ("pair", "core")
    blocks = lax.axis_size(grid)
    side = lax.axis_index("core")
    g = lax.axis_index(grid)
    case = ((g > 0).astype(jnp.int32) + (g == blocks - 1).astype(jnp.int32)).reshape(1)
    totals = jnp.asarray(totals_table(depth, height, width, blocks))
    upper = shifted(modes[:, :, :1], grid, -1)
    group = ("core", "mode")
    members = lax.axis_size(group)
    lanes = lax.axis_size("mode")
    first = element_pass(0, (modes, density, totals, eigenvalues, case), members, height, width, count)
    operands = (modes, upper, first, density, totals, eigenvalues, case)
    spread = element_pass(1, operands, members, height, width, count)
    got = lax.all_to_all(spread, group, 0, 0, tiled=False).astype(jnp.float32)
    sums = [(got[b * lanes] + got[b * lanes + 1]) + (got[b * lanes + 2] + got[b * lanes + 3]) for b in range(2)]
    own = jnp.where(side == 0, sums[0], sums[1])
    partner = jnp.where(side == 0, sums[1], sums[0])
    swap = [(b, b + 1) for b in range(1, blocks - 1, 2)] + [(b + 1, b) for b in range(1, blocks - 1, 2)]
    other = lax.ppermute(own.astype(jnp.bfloat16), grid, swap).astype(jnp.float32)
    low = jnp.where(side == 0, other, partner)
    high = jnp.where(side == 0, partner, other)
    widened = jnp.concatenate([low, own, high], 0)
    widened = jnp.pad(widened, ((0, 0), (2, 2), (0, 0)))
    return apply_stencil(widened, width)


def solution(mesh):
    devices = mesh.devices.reshape(mesh.devices.shape[0] // 2, 2, mesh.devices.shape[1])
    split = jax.sharding.Mesh(devices, ("pair", "core", "mode"))
    grid = ("pair", "core")
    in_specs = (P("mode", None, grid, None, None), P("mode"), P(grid, None, None))
    out_specs = P(grid, None, None)
    return jax.shard_map(local, mesh=split, in_specs=in_specs, out_specs=out_specs, check_vma=False)
```

```python
import functools

import jax
import jax.numpy as jnp
import ml_dtypes
import numpy as np
from jax import lax
from jax.experimental import pallas as pl
from jax.experimental.pallas import tpu as pltpu
from jax.sharding import PartitionSpec as P


def shifted(value, axis, steps):
    count = lax.axis_size(axis)
    first, last = (max(0, -steps), min(count, count - steps))
    return lax.ppermute(value, axis, [(source, source + steps) for source in range(first, last)])


def element_tables():
    poisson = 0.3
    lame_first = poisson / ((1.0 + poisson) * (1.0 - 2.0 * poisson))
    shear = 0.5 / (1.0 + poisson)
    elastic = np.zeros((6, 6))
    elastic[:3, :3] = lame_first
    for axis_bit in range(3):
        elastic[axis_bit, axis_bit] += 2.0 * shear
        elastic[axis_bit + 3, axis_bit + 3] = shear
    stiffness = np.zeros((24, 24))
    mass_small = np.zeros((8, 8))
    point = 1.0 / np.sqrt(3.0)
    for gauss in range(8):
        coords = [point * (2 * (gauss >> axis_bit & 1) - 1) for axis_bit in range(3)]
        shape_values = np.zeros(8)
        grads = np.zeros((3, 8))
        for corner in range(8):
            signs = [2 * (corner >> axis_bit & 1) - 1 for axis_bit in range(3)]
            factors = [1.0 + signs[axis_bit] * coords[axis_bit] for axis_bit in range(3)]
            shape_values[corner] = 0.125 * factors[0] * factors[1] * factors[2]
            grads[0, corner] = 0.25 * signs[0] * factors[1] * factors[2]
            grads[1, corner] = 0.25 * signs[1] * factors[0] * factors[2]
            grads[2, corner] = 0.25 * signs[2] * factors[0] * factors[1]
        strain = np.zeros((6, 24))
        for corner in range(8):
            column = 3 * corner
            strain[0, column] = grads[0, corner]
            strain[1, column + 1] = grads[1, corner]
            strain[2, column + 2] = grads[2, corner]
            strain[3, column] = grads[1, corner]
            strain[3, column + 1] = grads[0, corner]
            strain[4, column + 1] = grads[2, corner]
            strain[4, column + 2] = grads[1, corner]
            strain[5, column] = grads[2, corner]
            strain[5, column + 2] = grads[0, corner]
        stiffness = stiffness + strain.T @ elastic @ strain * 0.125
        mass_small = mass_small + np.outer(shape_values, shape_values) * 0.125
    mass = np.kron(mass_small, np.eye(3))
    return np.concatenate([stiffness, mass], 0).astype(np.float32)


def rounded_tables():
    table = element_tables().astype(ml_dtypes.bfloat16).astype(np.float32)
    return table[:24], table[24:]


def sector_tables():
    stiff_matrix, mass_matrix = rounded_tables()
    walsh = np.array([[(-1) ** bin(s & c).count("1") for c in range(8)] for s in range(8)], np.float64)
    full = np.kron(walsh, np.eye(3))
    back = full.T / 8.0
    assert np.array_equal(full @ back, np.eye(24))
    stiff = back.T @ stiff_matrix.astype(np.float64) @ back
    mass = back.T @ mass_matrix.astype(np.float64) @ back
    blocks = np.zeros((8, 3, 3))
    kept = np.zeros_like(stiff, bool)
    for e in range(8):
        for k in range(3):
            for q in range(3):
                i = 3 * (e ^ (1 << k)) + k
                j = 3 * (e ^ (1 << q)) + q
                blocks[e, k, q] = stiff[i, j]
                kept[i, j] = True
    assert not np.any(stiff[~kept])
    diagonal = np.diag(mass).reshape(8, 3)
    assert not np.any(mass - np.diag(np.diag(mass)))
    assert np.all(diagonal == diagonal[:, :1])
    return blocks, diagonal[:, 0]


def walsh(values):
    values = list(values)
    for bit in (1, 2, 4):
        for c in range(8):
            if c & bit == 0:
                a, b = values[c], values[c | bit]
                values[c], values[c | bit] = a + b, a - b
    return values


def element_forms(u, blocks, weights):
    spectra = [walsh([u[3 * c + k] for c in range(8)]) for k in range(3)]
    stiff = None
    for e in range(8):
        z = [spectra[k][e ^ (1 << k)] for k in range(3)]
        for k in range(3):
            term = None
            for q in range(k, 3):
                coefficient = blocks[e, k, q] * (1.0 if q == k else 2.0)
                if coefficient == 0.0:
                    continue
                piece = float(coefficient) * z[q]
                term = piece if term is None else term + piece
            if term is None:
                continue
            piece = z[k] * term
            stiff = piece if stiff is None else stiff + piece
    mass = None
    for s in range(8):
        power = spectra[0][s] * spectra[0][s] + spectra[1][s] * spectra[1][s] + spectra[2][s] * spectra[2][s]
        piece = float(weights[s]) * power
        mass = piece if mass is None else mass + piece
    return stiff, mass


def filter_offsets():
    listed = []
    for z_step in range(-2, 3):
        for y_step in range(-2, 3):
            for x_step in range(-2, 3):
                weight = 2.5 - float(np.sqrt(z_step * z_step + y_step * y_step + x_step * x_step))
                if weight > 0.0:
                    listed.append((z_step, y_step, x_step, weight))
    return listed


def totals_table(depth, height, width, blocks):
    listed = filter_offsets()
    out = []
    for first_layer in (0, depth, (blocks - 1) * depth):
        total = np.zeros((depth, height, width), np.float64)
        for z in range(depth):
            for z_step, y_step, x_step, weight in listed:
                layer = first_layer + z + z_step
                if layer < 0 or layer >= blocks * depth:
                    continue
                ys = np.arange(height) + y_step
                xs = np.arange(width) + x_step
                inside = ((ys >= 0) & (ys < height))[:, None] & ((xs >= 0) & (xs < width))[None, :]
                total[z] += weight * inside
        out.append(total)
    return np.stack(out).astype(np.float32)


def form_kernel(modes_ref, upper_ref, dens_ref, tot_ref, eig_ref, case_ref, out_ref, sh_ref):
    count = modes_ref.shape[0]
    depth = modes_ref.shape[2]
    height = modes_ref.shape[3]
    width = modes_ref.shape[4]
    blocks, weights = sector_tables()
    lane = lax.broadcasted_iota(jnp.int32, (height, width), 1)
    row = lax.broadcasted_iota(jnp.int32, (height, width), 0)
    x_edge = lane == width - 1
    y_edge = row == height - 1

    def plane(m, k, p):
        if p < depth:
            return modes_ref[m, k, p].astype(jnp.float32)
        return upper_ref[m, k, 0].astype(jnp.float32)

    def prepare(m, carry):
        for k in range(3):
            for p in range(depth + 1):
                base = plane(m, k, p)
                along_x = jnp.where(x_edge, 0.0, pltpu.roll(base, width - 1, 1))
                along_y = jnp.where(y_edge, 0.0, pltpu.roll(base, height - 1, 0))
                along_xy = jnp.where(y_edge, 0.0, pltpu.roll(along_x, height - 1, 0))
                sh_ref[m, k, p, 0] = base
                sh_ref[m, k, p, 1] = along_x
                sh_ref[m, k, p, 2] = along_y
                sh_ref[m, k, p, 3] = along_xy
        return carry

    lax.fori_loop(0, count, prepare, 0)

    chunks = height // 8

    def accumulate(m, carry):
        value = eig_ref[m]
        new = []
        for layer in range(depth):
            for b in range(chunks):
                rows = slice(8 * b, 8 * b + 8)
                u = []
                for corner in range(8):
                    x_off = corner & 1
                    y_off = corner >> 1 & 1
                    z_off = corner >> 2
                    for k in range(3):
                        u.append(sh_ref[m, k, layer + z_off, x_off + 2 * y_off, rows, :])
                stiff, mass = element_forms(u, blocks, weights)
                at = 2 * (layer * chunks + b)
                new.append(carry[at] + stiff)
                new.append(carry[at + 1] + value * mass)
        return tuple(new)

    zero = jnp.zeros((8, width), jnp.float32)
    sums = lax.fori_loop(0, count, accumulate, tuple(zero for _ in range(2 * depth * chunks)))
    case = case_ref[0]
    for layer in range(depth):
        for b in range(chunks):
            rows = slice(8 * b, 8 * b + 8)
            at = 2 * (layer * chunks + b)
            density = dens_ref[layer, rows, :]
            slope = 3.0 * (1.0 - 0.001) * density * density
            sensitivity = slope * sums[at] - sums[at + 1]
            scaled = (sensitivity / tot_ref[case, layer, rows, :]).astype(out_ref.dtype)
            for copy in range(out_ref.shape[0]):
                out_ref[copy, layer, rows, :] = scaled


def element_pass(operands, copies, depth, height, width, count):
    vmem = pl.BlockSpec(memory_space=pltpu.VMEM)
    smem = pl.BlockSpec(memory_space=pltpu.SMEM)
    specs = [vmem] * (len(operands) - 2) + [smem, smem]
    return pl.pallas_call(
        form_kernel,
        out_shape=jax.ShapeDtypeStruct((copies, depth, height, width), jnp.bfloat16),
        in_specs=specs,
        out_specs=vmem,
        scratch_shapes=[pltpu.VMEM((count, 3, depth + 1, 4, height, width), jnp.float32)],
    )(*operands)


def stencil_bands(width):
    offsets = []
    bands = []
    for z_step in range(-2, 3):
        for y_step in range(-2, 3):
            band = np.zeros((width, width), np.float32)
            used = False
            for x_step in range(-2, 3):
                weight = 2.5 - float(np.sqrt(z_step * z_step + y_step * y_step + x_step * x_step))
                if weight > 0.0:
                    band = band + weight * np.eye(width, k=-x_step, dtype=np.float32)
                    used = True
            if used:
                offsets.append((z_step, y_step))
                bands.append(band)
    return (offsets, np.stack(bands))


def apply_stencil(padded, width):
    depth = padded.shape[0] - 4
    height = padded.shape[1] - 4
    offsets, bands = stencil_bands(width)
    stacked = jnp.stack(
        [
            padded[2 + z_step : 2 + z_step + depth, 2 + y_step : 2 + y_step + height, :]
            for z_step, y_step in offsets
        ]
    )
    return jnp.einsum(
        "kzyx,kxw->zyw",
        stacked,
        jnp.asarray(bands),
        precision=lax.Precision.HIGHEST,
        preferred_element_type=jnp.float32,
    )


def local(modes, eigenvalues, density):
    count = modes.shape[0]
    depth = density.shape[0]
    height = density.shape[1]
    width = density.shape[2]
    grid = ("pair", "core")
    blocks = lax.axis_size(grid)
    side = lax.axis_index("core")
    g = lax.axis_index(grid)
    case = ((g > 0).astype(jnp.int32) + (g == blocks - 1).astype(jnp.int32)).reshape(1)
    totals = jnp.asarray(totals_table(depth, height, width, blocks))
    upper = shifted(modes[:, :, :1], grid, -1)
    group = ("core", "mode")
    members = lax.axis_size(group)
    lanes = lax.axis_size("mode")
    operands = (modes, upper, density, totals, eigenvalues, case)
    spread = element_pass(operands, members, depth, height, width, count)
    got = lax.all_to_all(spread, group, 0, 0, tiled=False).astype(jnp.float32)
    sums = [(got[b * lanes] + got[b * lanes + 1]) + (got[b * lanes + 2] + got[b * lanes + 3]) for b in range(2)]
    own = jnp.where(side == 0, sums[0], sums[1])
    partner = jnp.where(side == 0, sums[1], sums[0])
    swap = [(b, b + 1) for b in range(1, blocks - 1, 2)] + [(b + 1, b) for b in range(1, blocks - 1, 2)]
    other = lax.ppermute(own.astype(jnp.bfloat16), grid, swap).astype(jnp.float32)
    low = jnp.where(side == 0, other, partner)
    high = jnp.where(side == 0, partner, other)
    widened = jnp.concatenate([low, own, high], 0)
    widened = jnp.pad(widened, ((0, 0), (2, 2), (0, 0)))
    return apply_stencil(widened, width)


def solution(mesh):
    devices = mesh.devices.reshape(mesh.devices.shape[0] // 2, 2, mesh.devices.shape[1])
    split = jax.sharding.Mesh(devices, ("pair", "core", "mode"))
    grid = ("pair", "core")
    in_specs = (P("mode", None, grid, None, None), P("mode"), P(grid, None, None))
    out_specs = P(grid, None, None)
    return jax.shard_map(local, mesh=split, in_specs=in_specs, out_specs=out_specs, check_vma=False)
```

```python
import functools

import jax
import jax.numpy as jnp
import ml_dtypes
import numpy as np
from jax import lax
from jax.experimental import pallas as pl
from jax.experimental.pallas import tpu as pltpu
from jax.sharding import PartitionSpec as P


def shifted(value, axis, steps):
    count = lax.axis_size(axis)
    first, last = (max(0, -steps), min(count, count - steps))
    return lax.ppermute(value, axis, [(source, source + steps) for source in range(first, last)])


def element_tables():
    poisson = 0.3
    lame_first = poisson / ((1.0 + poisson) * (1.0 - 2.0 * poisson))
    shear = 0.5 / (1.0 + poisson)
    elastic = np.zeros((6, 6))
    elastic[:3, :3] = lame_first
    for axis_bit in range(3):
        elastic[axis_bit, axis_bit] += 2.0 * shear
        elastic[axis_bit + 3, axis_bit + 3] = shear
    stiffness = np.zeros((24, 24))
    mass_small = np.zeros((8, 8))
    point = 1.0 / np.sqrt(3.0)
    for gauss in range(8):
        coords = [point * (2 * (gauss >> axis_bit & 1) - 1) for axis_bit in range(3)]
        shape_values = np.zeros(8)
        grads = np.zeros((3, 8))
        for corner in range(8):
            signs = [2 * (corner >> axis_bit & 1) - 1 for axis_bit in range(3)]
            factors = [1.0 + signs[axis_bit] * coords[axis_bit] for axis_bit in range(3)]
            shape_values[corner] = 0.125 * factors[0] * factors[1] * factors[2]
            grads[0, corner] = 0.25 * signs[0] * factors[1] * factors[2]
            grads[1, corner] = 0.25 * signs[1] * factors[0] * factors[2]
            grads[2, corner] = 0.25 * signs[2] * factors[0] * factors[1]
        strain = np.zeros((6, 24))
        for corner in range(8):
            column = 3 * corner
            strain[0, column] = grads[0, corner]
            strain[1, column + 1] = grads[1, corner]
            strain[2, column + 2] = grads[2, corner]
            strain[3, column] = grads[1, corner]
            strain[3, column + 1] = grads[0, corner]
            strain[4, column + 1] = grads[2, corner]
            strain[4, column + 2] = grads[1, corner]
            strain[5, column] = grads[2, corner]
            strain[5, column + 2] = grads[0, corner]
        stiffness = stiffness + strain.T @ elastic @ strain * 0.125
        mass_small = mass_small + np.outer(shape_values, shape_values) * 0.125
    mass = np.kron(mass_small, np.eye(3))
    return np.concatenate([stiffness, mass], 0).astype(np.float32)


def rounded_tables():
    table = element_tables().astype(ml_dtypes.bfloat16).astype(np.float32)
    return table[:24], table[24:]


def sector_tables():
    stiff_matrix, mass_matrix = rounded_tables()
    walsh = np.array([[(-1) ** bin(s & c).count("1") for c in range(8)] for s in range(8)], np.float64)
    full = np.kron(walsh, np.eye(3))
    back = full.T / 8.0
    assert np.array_equal(full @ back, np.eye(24))
    stiff = back.T @ stiff_matrix.astype(np.float64) @ back
    mass = back.T @ mass_matrix.astype(np.float64) @ back
    blocks = np.zeros((8, 3, 3))
    kept = np.zeros_like(stiff, bool)
    for e in range(8):
        for k in range(3):
            for q in range(3):
                i = 3 * (e ^ (1 << k)) + k
                j = 3 * (e ^ (1 << q)) + q
                blocks[e, k, q] = stiff[i, j]
                kept[i, j] = True
    assert not np.any(stiff[~kept])
    diagonal = np.diag(mass).reshape(8, 3)
    assert not np.any(mass - np.diag(np.diag(mass)))
    assert np.all(diagonal == diagonal[:, :1])
    return blocks, diagonal[:, 0]


def walsh(values):
    values = list(values)
    for bit in (1, 2, 4):
        for c in range(8):
            if c & bit == 0:
                a, b = values[c], values[c | bit]
                values[c], values[c | bit] = a + b, a - b
    return values


def element_forms(u, blocks, weights):
    spectra = [walsh([u[3 * c + k] for c in range(8)]) for k in range(3)]
    return spectral_forms(spectra, blocks, weights)


def spectral_forms(spectra, blocks, weights):
    stiff = None
    for e in range(8):
        z = [spectra[k][e ^ (1 << k)] for k in range(3)]
        for k in range(3):
            term = None
            for q in range(k, 3):
                coefficient = blocks[e, k, q] * (1.0 if q == k else 2.0)
                if coefficient == 0.0:
                    continue
                piece = float(coefficient) * z[q]
                term = piece if term is None else term + piece
            if term is None:
                continue
            piece = z[k] * term
            stiff = piece if stiff is None else stiff + piece
    mass = None
    for s in range(8):
        power = spectra[0][s] * spectra[0][s] + spectra[1][s] * spectra[1][s] + spectra[2][s] * spectra[2][s]
        piece = float(weights[s]) * power
        mass = piece if mass is None else mass + piece
    return stiff, mass


def filter_offsets():
    listed = []
    for z_step in range(-2, 3):
        for y_step in range(-2, 3):
            for x_step in range(-2, 3):
                weight = 2.5 - float(np.sqrt(z_step * z_step + y_step * y_step + x_step * x_step))
                if weight > 0.0:
                    listed.append((z_step, y_step, x_step, weight))
    return listed


def totals_table(depth, height, width, blocks):
    listed = filter_offsets()
    out = []
    for first_layer in (0, depth, (blocks - 1) * depth):
        total = np.zeros((depth, height, width), np.float64)
        for z in range(depth):
            for z_step, y_step, x_step, weight in listed:
                layer = first_layer + z + z_step
                if layer < 0 or layer >= blocks * depth:
                    continue
                ys = np.arange(height) + y_step
                xs = np.arange(width) + x_step
                inside = ((ys >= 0) & (ys < height))[:, None] & ((xs >= 0) & (xs < width))[None, :]
                total[z] += weight * inside
        out.append(total)
    return np.stack(out).astype(np.float32)


def form_kernel(modes_ref, upper_ref, dens_ref, tot_ref, eig_ref, case_ref, out_ref, sh_ref):
    count = modes_ref.shape[0]
    depth = modes_ref.shape[2]
    height = modes_ref.shape[3]
    width = modes_ref.shape[4]
    blocks, weights = sector_tables()
    lane = lax.broadcasted_iota(jnp.int32, (height, width), 1)
    row = lax.broadcasted_iota(jnp.int32, (height, width), 0)
    x_edge = lane == width - 1
    y_edge = row == height - 1

    def plane(m, k, p):
        if p < depth:
            return modes_ref[m, k, p].astype(jnp.float32)
        return upper_ref[m, k, 0].astype(jnp.float32)

    def prepare(m, carry):
        for k in range(3):
            for p in range(depth + 1):
                base = plane(m, k, p)
                along_x = jnp.where(x_edge, 0.0, pltpu.roll(base, width - 1, 1))
                along_y = jnp.where(y_edge, 0.0, pltpu.roll(base, height - 1, 0))
                along_xy = jnp.where(y_edge, 0.0, pltpu.roll(along_x, height - 1, 0))
                sums_x = base + along_x
                diffs_x = base - along_x
                sums_xy = along_y + along_xy
                diffs_xy = along_y - along_xy
                sh_ref[m, k, p, 0] = sums_x + sums_xy
                sh_ref[m, k, p, 1] = diffs_x + diffs_xy
                sh_ref[m, k, p, 2] = sums_x - sums_xy
                sh_ref[m, k, p, 3] = diffs_x - diffs_xy
        return carry

    lax.fori_loop(0, count, prepare, 0)

    chunks = height // 8

    def accumulate(m, carry):
        value = eig_ref[m]
        new = []
        for layer in range(depth):
            for b in range(chunks):
                rows = slice(8 * b, 8 * b + 8)
                spectra = []
                for k in range(3):
                    below = [sh_ref[m, k, layer, v, rows, :] for v in range(4)]
                    above = [sh_ref[m, k, layer + 1, v, rows, :] for v in range(4)]
                    spectra.append([below[v] + above[v] for v in range(4)] + [below[v] - above[v] for v in range(4)])
                stiff, mass = spectral_forms(spectra, blocks, weights)
                at = 2 * (layer * chunks + b)
                new.append(carry[at] + stiff)
                new.append(carry[at + 1] + value * mass)
        return tuple(new)

    zero = jnp.zeros((8, width), jnp.float32)
    sums = lax.fori_loop(0, count, accumulate, tuple(zero for _ in range(2 * depth * chunks)))
    case = case_ref[0]
    for layer in range(depth):
        for b in range(chunks):
            rows = slice(8 * b, 8 * b + 8)
            at = 2 * (layer * chunks + b)
            density = dens_ref[layer, rows, :]
            slope = 3.0 * (1.0 - 0.001) * density * density
            sensitivity = slope * sums[at] - sums[at + 1]
            scaled = (sensitivity / tot_ref[case, layer, rows, :]).astype(out_ref.dtype)
            for copy in range(out_ref.shape[0]):
                out_ref[copy, layer, rows, :] = scaled


def element_pass(operands, copies, depth, height, width, count):
    vmem = pl.BlockSpec(memory_space=pltpu.VMEM)
    smem = pl.BlockSpec(memory_space=pltpu.SMEM)
    specs = [vmem] * (len(operands) - 2) + [smem, smem]
    return pl.pallas_call(
        form_kernel,
        out_shape=jax.ShapeDtypeStruct((copies, depth, height, width), jnp.bfloat16),
        in_specs=specs,
        out_specs=vmem,
        scratch_shapes=[pltpu.VMEM((count, 3, depth + 1, 4, height, width), jnp.float32)],
    )(*operands)


def stencil_bands(width):
    offsets = []
    bands = []
    for z_step in range(-2, 3):
        for y_step in range(-2, 3):
            band = np.zeros((width, width), np.float32)
            used = False
            for x_step in range(-2, 3):
                weight = 2.5 - float(np.sqrt(z_step * z_step + y_step * y_step + x_step * x_step))
                if weight > 0.0:
                    band = band + weight * np.eye(width, k=-x_step, dtype=np.float32)
                    used = True
            if used:
                offsets.append((z_step, y_step))
                bands.append(band)
    return (offsets, np.stack(bands))


def apply_stencil(padded, width):
    depth = padded.shape[0] - 4
    height = padded.shape[1] - 4
    offsets, bands = stencil_bands(width)
    stacked = jnp.stack(
        [
            padded[2 + z_step : 2 + z_step + depth, 2 + y_step : 2 + y_step + height, :]
            for z_step, y_step in offsets
        ]
    )
    return jnp.einsum(
        "kzyx,kxw->zyw",
        stacked,
        jnp.asarray(bands),
        precision=lax.Precision.HIGHEST,
        preferred_element_type=jnp.float32,
    )


def local(modes, eigenvalues, density):
    count = modes.shape[0]
    depth = density.shape[0]
    height = density.shape[1]
    width = density.shape[2]
    grid = ("pair", "core")
    blocks = lax.axis_size(grid)
    side = lax.axis_index("core")
    g = lax.axis_index(grid)
    case = ((g > 0).astype(jnp.int32) + (g == blocks - 1).astype(jnp.int32)).reshape(1)
    totals = jnp.asarray(totals_table(depth, height, width, blocks))
    upper = shifted(modes[:, :, :1], grid, -1)
    group = ("core", "mode")
    members = lax.axis_size(group)
    lanes = lax.axis_size("mode")
    operands = (modes, upper, density, totals, eigenvalues, case)
    spread = element_pass(operands, members, depth, height, width, count)
    got = lax.all_to_all(spread, group, 0, 0, tiled=False).astype(jnp.float32)
    sums = [(got[b * lanes] + got[b * lanes + 1]) + (got[b * lanes + 2] + got[b * lanes + 3]) for b in range(2)]
    own = jnp.where(side == 0, sums[0], sums[1])
    partner = jnp.where(side == 0, sums[1], sums[0])
    swap = [(b, b + 1) for b in range(1, blocks - 1, 2)] + [(b + 1, b) for b in range(1, blocks - 1, 2)]
    other = lax.ppermute(own.astype(jnp.bfloat16), grid, swap).astype(jnp.float32)
    low = jnp.where(side == 0, other, partner)
    high = jnp.where(side == 0, partner, other)
    widened = jnp.concatenate([low, own, high], 0)
    widened = jnp.pad(widened, ((0, 0), (2, 2), (0, 0)))
    return apply_stencil(widened, width)


def solution(mesh):
    devices = mesh.devices.reshape(mesh.devices.shape[0] // 2, 2, mesh.devices.shape[1])
    split = jax.sharding.Mesh(devices, ("pair", "core", "mode"))
    grid = ("pair", "core")
    in_specs = (P("mode", None, grid, None, None), P("mode"), P(grid, None, None))
    out_specs = P(grid, None, None)
    return jax.shard_map(local, mesh=split, in_specs=in_specs, out_specs=out_specs, check_vma=False)
```

```python
import functools

import jax
import jax.numpy as jnp
import ml_dtypes
import numpy as np
from jax import lax
from jax.experimental import pallas as pl
from jax.experimental.pallas import tpu as pltpu
from jax.sharding import PartitionSpec as P


def shifted(value, axis, steps):
    count = lax.axis_size(axis)
    first, last = (max(0, -steps), min(count, count - steps))
    return lax.ppermute(value, axis, [(source, source + steps) for source in range(first, last)])


def element_tables():
    poisson = 0.3
    lame_first = poisson / ((1.0 + poisson) * (1.0 - 2.0 * poisson))
    shear = 0.5 / (1.0 + poisson)
    elastic = np.zeros((6, 6))
    elastic[:3, :3] = lame_first
    for axis_bit in range(3):
        elastic[axis_bit, axis_bit] += 2.0 * shear
        elastic[axis_bit + 3, axis_bit + 3] = shear
    stiffness = np.zeros((24, 24))
    mass_small = np.zeros((8, 8))
    point = 1.0 / np.sqrt(3.0)
    for gauss in range(8):
        coords = [point * (2 * (gauss >> axis_bit & 1) - 1) for axis_bit in range(3)]
        shape_values = np.zeros(8)
        grads = np.zeros((3, 8))
        for corner in range(8):
            signs = [2 * (corner >> axis_bit & 1) - 1 for axis_bit in range(3)]
            factors = [1.0 + signs[axis_bit] * coords[axis_bit] for axis_bit in range(3)]
            shape_values[corner] = 0.125 * factors[0] * factors[1] * factors[2]
            grads[0, corner] = 0.25 * signs[0] * factors[1] * factors[2]
            grads[1, corner] = 0.25 * signs[1] * factors[0] * factors[2]
            grads[2, corner] = 0.25 * signs[2] * factors[0] * factors[1]
        strain = np.zeros((6, 24))
        for corner in range(8):
            column = 3 * corner
            strain[0, column] = grads[0, corner]
            strain[1, column + 1] = grads[1, corner]
            strain[2, column + 2] = grads[2, corner]
            strain[3, column] = grads[1, corner]
            strain[3, column + 1] = grads[0, corner]
            strain[4, column + 1] = grads[2, corner]
            strain[4, column + 2] = grads[1, corner]
            strain[5, column] = grads[2, corner]
            strain[5, column + 2] = grads[0, corner]
        stiffness = stiffness + strain.T @ elastic @ strain * 0.125
        mass_small = mass_small + np.outer(shape_values, shape_values) * 0.125
    mass = np.kron(mass_small, np.eye(3))
    return np.concatenate([stiffness, mass], 0).astype(np.float32)


def rounded_tables():
    table = element_tables().astype(ml_dtypes.bfloat16).astype(np.float32)
    return table[:24], table[24:]


def sector_tables():
    stiff_matrix, mass_matrix = rounded_tables()
    walsh = np.array([[(-1) ** bin(s & c).count("1") for c in range(8)] for s in range(8)], np.float64)
    full = np.kron(walsh, np.eye(3))
    back = full.T / 8.0
    assert np.array_equal(full @ back, np.eye(24))
    stiff = back.T @ stiff_matrix.astype(np.float64) @ back
    mass = back.T @ mass_matrix.astype(np.float64) @ back
    blocks = np.zeros((8, 3, 3))
    kept = np.zeros_like(stiff, bool)
    for e in range(8):
        for k in range(3):
            for q in range(3):
                i = 3 * (e ^ (1 << k)) + k
                j = 3 * (e ^ (1 << q)) + q
                blocks[e, k, q] = stiff[i, j]
                kept[i, j] = True
    assert not np.any(stiff[~kept])
    diagonal = np.diag(mass).reshape(8, 3)
    assert not np.any(mass - np.diag(np.diag(mass)))
    assert np.all(diagonal == diagonal[:, :1])
    return blocks, diagonal[:, 0]


def walsh(values):
    values = list(values)
    for bit in (1, 2, 4):
        for c in range(8):
            if c & bit == 0:
                a, b = values[c], values[c | bit]
                values[c], values[c | bit] = a + b, a - b
    return values


def element_forms(u, blocks, weights):
    spectra = [walsh([u[3 * c + k] for c in range(8)]) for k in range(3)]
    stiff = None
    for e in range(8):
        z = [spectra[k][e ^ (1 << k)] for k in range(3)]
        for k in range(3):
            term = None
            for q in range(k, 3):
                coefficient = blocks[e, k, q] * (1.0 if q == k else 2.0)
                if coefficient == 0.0:
                    continue
                piece = float(coefficient) * z[q]
                term = piece if term is None else term + piece
            if term is None:
                continue
            piece = z[k] * term
            stiff = piece if stiff is None else stiff + piece
    mass = None
    for s in range(8):
        power = spectra[0][s] * spectra[0][s] + spectra[1][s] * spectra[1][s] + spectra[2][s] * spectra[2][s]
        piece = float(weights[s]) * power
        mass = piece if mass is None else mass + piece
    return stiff, mass


def filter_offsets():
    listed = []
    for z_step in range(-2, 3):
        for y_step in range(-2, 3):
            for x_step in range(-2, 3):
                weight = 2.5 - float(np.sqrt(z_step * z_step + y_step * y_step + x_step * x_step))
                if weight > 0.0:
                    listed.append((z_step, y_step, x_step, weight))
    return listed


def totals_table(depth, height, width, blocks):
    listed = filter_offsets()
    out = []
    for first_layer in (0, depth, (blocks - 1) * depth):
        total = np.zeros((depth, height, width), np.float64)
        for z in range(depth):
            for z_step, y_step, x_step, weight in listed:
                layer = first_layer + z + z_step
                if layer < 0 or layer >= blocks * depth:
                    continue
                ys = np.arange(height) + y_step
                xs = np.arange(width) + x_step
                inside = ((ys >= 0) & (ys < height))[:, None] & ((xs >= 0) & (xs < width))[None, :]
                total[z] += weight * inside
        out.append(total)
    return np.stack(out).astype(np.float32)


def form_kernel(modes_ref, upper_ref, dens_ref, tot_ref, eig_ref, case_ref, out_ref, sh_ref):
    count = modes_ref.shape[0]
    depth = modes_ref.shape[2]
    height = modes_ref.shape[3]
    width = modes_ref.shape[4]
    blocks, weights = sector_tables()
    lane = lax.broadcasted_iota(jnp.int32, (height, width), 1)
    row = lax.broadcasted_iota(jnp.int32, (height, width), 0)
    x_edge = lane == width - 1
    y_edge = row == height - 1

    def plane(m, k, p):
        if p < depth:
            return modes_ref[m, k, p].astype(jnp.float32)
        return upper_ref[m, k, 0].astype(jnp.float32)

    def prepare(m, carry):
        for k in range(3):
            for p in range(depth + 1):
                base = plane(m, k, p)
                along_x = jnp.where(x_edge, 0.0, pltpu.roll(base, width - 1, 1))
                along_y = jnp.where(y_edge, 0.0, pltpu.roll(base, height - 1, 0))
                along_xy = jnp.where(y_edge, 0.0, pltpu.roll(along_x, height - 1, 0))
                sh_ref[m, k, p, 0] = base
                sh_ref[m, k, p, 1] = along_x
                sh_ref[m, k, p, 2] = along_y
                sh_ref[m, k, p, 3] = along_xy
        return carry

    lax.fori_loop(0, count, prepare, 0)

    chunks = height // 8

    def accumulate(m, carry):
        value = eig_ref[m]
        new = []
        for layer in range(depth):
            for b in range(chunks):
                rows = slice(8 * b, 8 * b + 8)
                u = []
                for corner in range(8):
                    x_off = corner & 1
                    y_off = corner >> 1 & 1
                    z_off = corner >> 2
                    for k in range(3):
                        u.append(sh_ref[m, k, layer + z_off, x_off + 2 * y_off, rows, :])
                stiff, mass = element_forms(u, blocks, weights)
                at = 2 * (layer * chunks + b)
                new.append(carry[at] + stiff)
                new.append(carry[at + 1] + value * mass)
        return tuple(new)

    zero = jnp.zeros((8, width), jnp.float32)
    sums = lax.fori_loop(0, count, accumulate, tuple(zero for _ in range(2 * depth * chunks)))
    case = case_ref[0]
    for layer in range(depth):
        for b in range(chunks):
            rows = slice(8 * b, 8 * b + 8)
            at = 2 * (layer * chunks + b)
            density = dens_ref[layer, rows, :]
            slope = 3.0 * (1.0 - 0.001) * density * density
            sensitivity = slope * sums[at] - sums[at + 1]
            scaled = (sensitivity / tot_ref[case, layer, rows, :]).astype(out_ref.dtype)
            for copy in range(out_ref.shape[0]):
                out_ref[copy, layer, rows, :] = scaled


def element_pass(operands, copies, depth, height, width, count):
    vmem = pl.BlockSpec(memory_space=pltpu.VMEM)
    smem = pl.BlockSpec(memory_space=pltpu.SMEM)
    specs = [vmem] * (len(operands) - 2) + [smem, smem]
    return pl.pallas_call(
        form_kernel,
        out_shape=jax.ShapeDtypeStruct((copies, depth, height, width), jnp.bfloat16),
        in_specs=specs,
        out_specs=vmem,
        scratch_shapes=[pltpu.VMEM((count, 3, depth + 1, 4, height, width), jnp.float32)],
    )(*operands)


def stencil_bands(width):
    offsets = []
    bands = []
    for z_step in range(-2, 3):
        for y_step in range(-2, 3):
            band = np.zeros((width, width), np.float32)
            used = False
            for x_step in range(-2, 3):
                weight = 2.5 - float(np.sqrt(z_step * z_step + y_step * y_step + x_step * x_step))
                if weight > 0.0:
                    band = band + weight * np.eye(width, k=-x_step, dtype=np.float32)
                    used = True
            if used:
                offsets.append((z_step, y_step))
                bands.append(band)
    return (offsets, np.stack(bands))


def apply_stencil(padded, width):
    depth = padded.shape[0] - 4
    height = padded.shape[1] - 4
    offsets, bands = stencil_bands(width)
    stacked = jnp.stack(
        [
            padded[2 + z_step : 2 + z_step + depth, 2 + y_step : 2 + y_step + height, :]
            for z_step, y_step in offsets
        ]
    )
    return jnp.einsum(
        "kzyx,kxw->zyw",
        stacked,
        jnp.asarray(bands),
        precision=lax.Precision.HIGHEST,
        preferred_element_type=jnp.float32,
    )


def local(modes, eigenvalues, density):
    count = modes.shape[0]
    depth = density.shape[0]
    height = density.shape[1]
    width = density.shape[2]
    grid = ("pair", "core")
    blocks = lax.axis_size(grid)
    side = lax.axis_index("core")
    g = lax.axis_index(grid)
    case = ((g > 0).astype(jnp.int32) + (g == blocks - 1).astype(jnp.int32)).reshape(1)
    totals = jnp.asarray(totals_table(depth, height, width, blocks))
    upper = shifted(modes[:, :, :1], grid, -1)
    group = ("core", "mode")
    members = lax.axis_size(group)
    lanes = lax.axis_size("mode")
    operands = (modes, upper, density, totals, eigenvalues, case)
    spread = element_pass(operands, members, depth, height, width, count)
    got = lax.all_to_all(spread, group, 0, 0, tiled=False).astype(jnp.float32)
    sums = [(got[b * lanes] + got[b * lanes + 1]) + (got[b * lanes + 2] + got[b * lanes + 3]) for b in range(2)]
    own = jnp.where(side == 0, sums[0], sums[1])
    partner = jnp.where(side == 0, sums[1], sums[0])
    swap = [(b, b + 1) for b in range(1, blocks - 1, 2)] + [(b + 1, b) for b in range(1, blocks - 1, 2)]
    other = lax.ppermute(own.astype(jnp.bfloat16), grid, swap)
    zero = jnp.zeros_like(own)
    local_low = jnp.where(side == 0, zero, partner)
    local_high = jnp.where(side == 0, partner, zero)
    widened = jnp.concatenate([local_low, own, local_high], 0)
    widened = jnp.pad(widened, ((0, 0), (2, 2), (0, 0)))
    inner = lax.optimization_barrier(apply_stencil(widened, width))
    nothing = jnp.zeros_like(other)
    far_low = jnp.where(side == 0, other, nothing)
    far_high = jnp.where(side == 0, nothing, other)
    return inner + halo_stencil(far_low, far_high, width)


def halo_stencil(low, high, width):
    depth = low.shape[0]
    height = low.shape[1]
    around = jnp.pad(jnp.concatenate([low, high], 0), ((0, 0), (2, 2), (0, 0)))
    pieces = []
    bands = []
    for z in range(depth):
        for source in range(2 * depth):
            layer = source - depth if source < depth else source
            z_step = layer - z
            for y_step in range(-2, 3):
                band = np.zeros((width, width), np.float32)
                used = False
                for x_step in range(-2, 3):
                    weight = 2.5 - float(np.sqrt(z_step * z_step + y_step * y_step + x_step * x_step))
                    if weight > 0.0:
                        band = band + weight * np.eye(width, k=-x_step, dtype=np.float32)
                        used = True
                if used:
                    pieces.append((z, source, y_step))
                    bands.append(band)
    rows = []
    for z in range(depth):
        chosen = [i for i, piece in enumerate(pieces) if piece[0] == z]
        stacked = jnp.stack([around[pieces[i][1], 2 + pieces[i][2] : 2 + pieces[i][2] + height] for i in chosen])
        rows.append(
            jnp.einsum(
                "kyx,kxw->yw",
                stacked,
                jnp.asarray(np.stack([bands[i] for i in chosen])),
                precision=lax.Precision.HIGH,
                preferred_element_type=jnp.float32,
            )
        )
    return jnp.stack(rows)


def solution(mesh):
    devices = mesh.devices.reshape(mesh.devices.shape[0] // 2, 2, mesh.devices.shape[1])
    split = jax.sharding.Mesh(devices, ("pair", "core", "mode"))
    grid = ("pair", "core")
    in_specs = (P("mode", None, grid, None, None), P("mode"), P(grid, None, None))
    out_specs = P(grid, None, None)
    return jax.shard_map(local, mesh=split, in_specs=in_specs, out_specs=out_specs, check_vma=False)
```

```python
import functools

import jax
import jax.numpy as jnp
import ml_dtypes
import numpy as np
from jax import lax
from jax.experimental import pallas as pl
from jax.experimental.pallas import tpu as pltpu
from jax.sharding import PartitionSpec as P


def shifted(value, axis, steps):
    count = lax.axis_size(axis)
    first, last = (max(0, -steps), min(count, count - steps))
    return lax.ppermute(value, axis, [(source, source + steps) for source in range(first, last)])


def element_tables():
    poisson = 0.3
    lame_first = poisson / ((1.0 + poisson) * (1.0 - 2.0 * poisson))
    shear = 0.5 / (1.0 + poisson)
    elastic = np.zeros((6, 6))
    elastic[:3, :3] = lame_first
    for axis_bit in range(3):
        elastic[axis_bit, axis_bit] += 2.0 * shear
        elastic[axis_bit + 3, axis_bit + 3] = shear
    stiffness = np.zeros((24, 24))
    mass_small = np.zeros((8, 8))
    point = 1.0 / np.sqrt(3.0)
    for gauss in range(8):
        coords = [point * (2 * (gauss >> axis_bit & 1) - 1) for axis_bit in range(3)]
        shape_values = np.zeros(8)
        grads = np.zeros((3, 8))
        for corner in range(8):
            signs = [2 * (corner >> axis_bit & 1) - 1 for axis_bit in range(3)]
            factors = [1.0 + signs[axis_bit] * coords[axis_bit] for axis_bit in range(3)]
            shape_values[corner] = 0.125 * factors[0] * factors[1] * factors[2]
            grads[0, corner] = 0.25 * signs[0] * factors[1] * factors[2]
            grads[1, corner] = 0.25 * signs[1] * factors[0] * factors[2]
            grads[2, corner] = 0.25 * signs[2] * factors[0] * factors[1]
        strain = np.zeros((6, 24))
        for corner in range(8):
            column = 3 * corner
            strain[0, column] = grads[0, corner]
            strain[1, column + 1] = grads[1, corner]
            strain[2, column + 2] = grads[2, corner]
            strain[3, column] = grads[1, corner]
            strain[3, column + 1] = grads[0, corner]
            strain[4, column + 1] = grads[2, corner]
            strain[4, column + 2] = grads[1, corner]
            strain[5, column] = grads[2, corner]
            strain[5, column + 2] = grads[0, corner]
        stiffness = stiffness + strain.T @ elastic @ strain * 0.125
        mass_small = mass_small + np.outer(shape_values, shape_values) * 0.125
    mass = np.kron(mass_small, np.eye(3))
    return np.concatenate([stiffness, mass], 0).astype(np.float32)


def rounded_tables():
    table = element_tables().astype(ml_dtypes.bfloat16).astype(np.float32)
    return table[:24], table[24:]


def sector_tables():
    stiff_matrix, mass_matrix = rounded_tables()
    walsh = np.array([[(-1) ** bin(s & c).count("1") for c in range(8)] for s in range(8)], np.float64)
    full = np.kron(walsh, np.eye(3))
    back = full.T / 8.0
    assert np.array_equal(full @ back, np.eye(24))
    stiff = back.T @ stiff_matrix.astype(np.float64) @ back
    mass = back.T @ mass_matrix.astype(np.float64) @ back
    blocks = np.zeros((8, 3, 3))
    kept = np.zeros_like(stiff, bool)
    for e in range(8):
        for k in range(3):
            for q in range(3):
                i = 3 * (e ^ (1 << k)) + k
                j = 3 * (e ^ (1 << q)) + q
                blocks[e, k, q] = stiff[i, j]
                kept[i, j] = True
    assert not np.any(stiff[~kept])
    diagonal = np.diag(mass).reshape(8, 3)
    assert not np.any(mass - np.diag(np.diag(mass)))
    assert np.all(diagonal == diagonal[:, :1])
    return blocks, diagonal[:, 0]


def walsh(values):
    values = list(values)
    for bit in (1, 2, 4):
        for c in range(8):
            if c & bit == 0:
                a, b = values[c], values[c | bit]
                values[c], values[c | bit] = a + b, a - b
    return values


def element_forms(u, blocks, weights):
    spectra = [walsh([u[3 * c + k] for c in range(8)]) for k in range(3)]
    stiff = None
    for e in range(8):
        z = [spectra[k][e ^ (1 << k)] for k in range(3)]
        for k in range(3):
            term = None
            for q in range(k, 3):
                coefficient = blocks[e, k, q] * (1.0 if q == k else 2.0)
                if coefficient == 0.0:
                    continue
                piece = float(coefficient) * z[q]
                term = piece if term is None else term + piece
            if term is None:
                continue
            piece = z[k] * term
            stiff = piece if stiff is None else stiff + piece
    mass = None
    for s in range(8):
        power = spectra[0][s] * spectra[0][s] + spectra[1][s] * spectra[1][s] + spectra[2][s] * spectra[2][s]
        piece = float(weights[s]) * power
        mass = piece if mass is None else mass + piece
    return stiff, mass


def filter_offsets():
    listed = []
    for z_step in range(-2, 3):
        for y_step in range(-2, 3):
            for x_step in range(-2, 3):
                weight = 2.5 - float(np.sqrt(z_step * z_step + y_step * y_step + x_step * x_step))
                if weight > 0.0:
                    listed.append((z_step, y_step, x_step, weight))
    return listed


def totals_table(depth, height, width, blocks):
    listed = filter_offsets()
    out = []
    for first_layer in (0, depth, (blocks - 1) * depth):
        total = np.zeros((depth, height, width), np.float64)
        for z in range(depth):
            for z_step, y_step, x_step, weight in listed:
                layer = first_layer + z + z_step
                if layer < 0 or layer >= blocks * depth:
                    continue
                ys = np.arange(height) + y_step
                xs = np.arange(width) + x_step
                inside = ((ys >= 0) & (ys < height))[:, None] & ((xs >= 0) & (xs < width))[None, :]
                total[z] += weight * inside
        out.append(total)
    return np.stack(out).astype(np.float32)


def form_kernel(modes_ref, upper_ref, dens_ref, tot_ref, eig_ref, case_ref, out_ref, sh_ref):
    count = modes_ref.shape[0]
    depth = modes_ref.shape[2]
    height = modes_ref.shape[3]
    width = modes_ref.shape[4]
    blocks, weights = sector_tables()
    lane = lax.broadcasted_iota(jnp.int32, (height, width), 1)
    row = lax.broadcasted_iota(jnp.int32, (height, width), 0)
    x_edge = lane == width - 1
    y_edge = row == height - 1

    def plane(m, k, p):
        if p < depth:
            return modes_ref[m, k, p].astype(jnp.float32)
        return upper_ref[m, k, 0].astype(jnp.float32)

    def prepare(m, carry):
        for k in range(3):
            for p in range(depth + 1):
                base = plane(m, k, p)
                along_x = jnp.where(x_edge, 0.0, pltpu.roll(base, width - 1, 1))
                along_y = jnp.where(y_edge, 0.0, pltpu.roll(base, height - 1, 0))
                along_xy = jnp.where(y_edge, 0.0, pltpu.roll(along_x, height - 1, 0))
                sh_ref[m, k, p, 0] = base
                sh_ref[m, k, p, 1] = along_x
                sh_ref[m, k, p, 2] = along_y
                sh_ref[m, k, p, 3] = along_xy
        return carry

    lax.fori_loop(0, count, prepare, 0)

    chunks = height // 8

    def accumulate(m, carry):
        value = eig_ref[m]
        new = []
        for layer in range(depth):
            for b in range(chunks):
                rows = slice(8 * b, 8 * b + 8)
                u = []
                for corner in range(8):
                    x_off = corner & 1
                    y_off = corner >> 1 & 1
                    z_off = corner >> 2
                    for k in range(3):
                        u.append(sh_ref[m, k, layer + z_off, x_off + 2 * y_off, rows, :])
                stiff, mass = element_forms(u, blocks, weights)
                at = 2 * (layer * chunks + b)
                new.append(carry[at] + stiff)
                new.append(carry[at + 1] + value * mass)
        return tuple(new)

    zero = jnp.zeros((8, width), jnp.float32)
    sums = lax.fori_loop(0, count, accumulate, tuple(zero for _ in range(2 * depth * chunks)))
    case = case_ref[0]
    for layer in range(depth):
        for b in range(chunks):
            rows = slice(8 * b, 8 * b + 8)
            at = 2 * (layer * chunks + b)
            density = dens_ref[layer, rows, :]
            slope = 3.0 * (1.0 - 0.001) * density * density
            sensitivity = slope * sums[at] - sums[at + 1]
            scaled = (sensitivity / tot_ref[case, layer, rows, :]).astype(out_ref.dtype)
            for copy in range(out_ref.shape[0]):
                out_ref[copy, layer, rows, :] = scaled


def element_pass(operands, copies, depth, height, width, count):
    vmem = pl.BlockSpec(memory_space=pltpu.VMEM)
    smem = pl.BlockSpec(memory_space=pltpu.SMEM)
    specs = [vmem] * (len(operands) - 2) + [smem, smem]
    return pl.pallas_call(
        form_kernel,
        out_shape=jax.ShapeDtypeStruct((copies, depth, height, width), jnp.bfloat16),
        in_specs=specs,
        out_specs=vmem,
        scratch_shapes=[pltpu.VMEM((count, 3, depth + 1, 4, height, width), jnp.float32)],
    )(*operands)


def stencil_bands(width):
    offsets = []
    bands = []
    for z_step in range(-2, 3):
        for y_step in range(-2, 3):
            band = np.zeros((width, width), np.float32)
            used = False
            for x_step in range(-2, 3):
                weight = 2.5 - float(np.sqrt(z_step * z_step + y_step * y_step + x_step * x_step))
                if weight > 0.0:
                    band = band + weight * np.eye(width, k=-x_step, dtype=np.float32)
                    used = True
            if used:
                offsets.append((z_step, y_step))
                bands.append(band)
    return (offsets, np.stack(bands))


def apply_stencil(padded, width):
    depth = padded.shape[0] - 4
    height = padded.shape[1] - 4
    offsets, bands = stencil_bands(width)
    stacked = jnp.stack(
        [
            padded[2 + z_step : 2 + z_step + depth, 2 + y_step : 2 + y_step + height, :]
            for z_step, y_step in offsets
        ]
    )
    return jnp.einsum(
        "kzyx,kxw->zyw",
        stacked,
        jnp.asarray(bands),
        precision=lax.Precision.HIGHEST,
        preferred_element_type=jnp.float32,
    )


def local(modes, eigenvalues, density):
    count = modes.shape[0]
    depth = density.shape[0]
    height = density.shape[1]
    width = density.shape[2]
    grid = ("pair", "core")
    blocks = lax.axis_size(grid)
    side = lax.axis_index("core")
    g = lax.axis_index(grid)
    case = ((g > 0).astype(jnp.int32) + (g == blocks - 1).astype(jnp.int32)).reshape(1)
    totals = jnp.asarray(totals_table(depth, height, width, blocks))
    upper = shifted(modes[:, :, :1], grid, -1)
    group = ("core", "mode")
    members = lax.axis_size(group)
    lanes = lax.axis_size("mode")
    operands = (modes, upper, density, totals, eigenvalues, case)
    spread = element_pass(operands, members, depth, height, width, count)
    got = lax.all_to_all(spread, group, 0, 0, tiled=False).astype(jnp.float32)
    sums = [(got[b * lanes] + got[b * lanes + 1]) + (got[b * lanes + 2] + got[b * lanes + 3]) for b in range(2)]
    own = jnp.where(side == 0, sums[0], sums[1])
    partner = jnp.where(side == 0, sums[1], sums[0])
    swap = [(b, b + 1) for b in range(1, blocks - 1, 2)] + [(b + 1, b) for b in range(1, blocks - 1, 2)]
    other = lax.ppermute(own.astype(jnp.bfloat16), grid, swap)
    zero = jnp.zeros_like(own)
    local_low = jnp.where(side == 0, zero, partner)
    local_high = jnp.where(side == 0, partner, zero)
    widened = jnp.concatenate([local_low, own, local_high], 0)
    widened = jnp.pad(widened, ((0, 0), (2, 2), (0, 0)))
    inner = lax.optimization_barrier(apply_stencil(widened, width))
    nothing = jnp.zeros_like(other)
    far_low = jnp.where(side == 0, other, nothing)
    far_high = jnp.where(side == 0, nothing, other)
    return inner + halo_stencil(far_low, far_high, width)


def halo_stencil(low, high, width):
    depth = low.shape[0]
    height = low.shape[1]
    around = jnp.pad(jnp.concatenate([low, high], 0), ((0, 0), (2, 2), (0, 0)))
    pieces = []
    bands = []
    for z in range(depth):
        for source in range(2 * depth):
            layer = source - depth if source < depth else source
            z_step = layer - z
            for y_step in range(-2, 3):
                band = np.zeros((width, width), np.float32)
                used = False
                for x_step in range(-2, 3):
                    weight = 2.5 - float(np.sqrt(z_step * z_step + y_step * y_step + x_step * x_step))
                    if weight > 0.0:
                        band = band + weight * np.eye(width, k=-x_step, dtype=np.float32)
                        used = True
                if used:
                    pieces.append((z, source, y_step))
                    bands.append(band)
    stacked = []
    for z, source, y_step in pieces:
        piece = around[source, 2 + y_step : 2 + y_step + height]
        stacked.append(jnp.stack([piece if layer == z else jnp.zeros_like(piece) for layer in range(depth)]))
    return jnp.einsum(
        "kzyx,kxw->zyw",
        jnp.stack(stacked),
        jnp.asarray(np.stack(bands)),
        precision=lax.Precision.HIGH,
        preferred_element_type=jnp.float32,
    )


def solution(mesh):
    devices = mesh.devices.reshape(mesh.devices.shape[0] // 2, 2, mesh.devices.shape[1])
    split = jax.sharding.Mesh(devices, ("pair", "core", "mode"))
    grid = ("pair", "core")
    in_specs = (P("mode", None, grid, None, None), P("mode"), P(grid, None, None))
    out_specs = P(grid, None, None)
    return jax.shard_map(local, mesh=split, in_specs=in_specs, out_specs=out_specs, check_vma=False)
```
